256 devices in a mesh: row: 16 (over z, core), col: 16 (over y, x).
Axes of the slice: x: 4, y: 4, z: 8, core: 2. Of those that a mesh axis runs over, the one named last changes fastest.
Arguments:
- prior_window_motion: float32 [3, 128, 128, 256], P(None, 'row', 'col'), may hold values from -1.2 to 1.2
- prior_window_stress: float32 [128, 128, 256], P('row', 'col'), may hold values from -3 to 3
- heat_scalar: float32 [128, 128, 256], P('row', 'col'), may hold values from 0 to 1
Outputs:
- velocity: float32 [3, 128, 128, 256], P(None, 'row', 'col')
- pressure: float32 [128, 128, 256], P('row', 'col')
The draws below stay inside these ranges and needn't reach their ends.
All inputs are finite; a program needn't handle non-finite values.
Results may differ from the reference program's by a relative error of at most 0.0003.
Values sent between devices are 32-bit elements; how exact they have to be, the bound alone decides.
No kernel may reach another device: no remote copies, remote signals or barrier semaphores. Data moves between devices by JAX's collectives and lax.ppermute only.
A program may use at most 64 MiB of HBM per device.

```python
import jax
import jax.numpy as jnp

NX = 256
OUTER = 2
INNER = 2
NY = 128
NZ = 128


def draw_heat_scalar(key, part):
    uniform_noise = jax.random.uniform(key, (NY, NZ, NX), jnp.float32)
    ycoord = (jnp.arange(NY, dtype=jnp.float32) / NY)[:, None, None]
    zcoord = (jnp.arange(NZ, dtype=jnp.float32) / NZ)[None, :, None]
    amplitude = 0.25 + 0.375 * (ycoord + zcoord)
    return 0.5 + amplitude * (uniform_noise - 0.5)


def levels(key, shape, shards, smallest, largest):
    factor_of, own = 1.0, jax.random.fold_in(key, 6)
    for position, blocks in shards:
        draws = jnp.exp(jax.random.uniform(jax.random.fold_in(own, position), (blocks,), jnp.float32, smallest / len(shards), largest / len(shards)))
        factor_of = factor_of * jnp.repeat(draws, shape[position] // blocks).reshape([-1 if axis == position else 1 for axis in range(len(shape))])
    return factor_of


def noise(rng, shape, scale, bound, shards=(), kind=jnp.bfloat16):
    drawn = jax.random.normal(rng, shape, jnp.float32) * scale
    if len(shards) > 0:
        drawn = levels(rng, shape, shards, -0.22, 0.18) * drawn
    return jnp.clip(drawn, min=-bound, max=bound).astype(kind)


def setup_inputs(seed: int = 0) -> dict:
    streams_of = jax.random.split(jax.random.key(seed), 4)
    return {
        "prior_window_motion": noise(streams_of[0], (3, NY, NZ, NX), 0.2, 1.2, ((1, 16), (2, 16)), jnp.float32),
        "prior_window_stress": noise(streams_of[1], (NY, NZ, NX), 0.5, 3.0, ((0, 16), (1, 16)), jnp.float32),
        "heat_scalar": draw_heat_scalar(jax.random.fold_in(streams_of[3], 71), 0),
    }


ENABLE_SWITCH = 2.0
OFFSET_COUNT = 0.5
AUGMENT = 1.0
ANCHOR = 0.002
RAYLEIGH_NUMBER = 1.0
SMOOTHING = 2.0
SPATIAL = (2, 0, 1)


def forward_diff(field, axis_index):
    return jnp.roll(field, -1, axis_index) - field


def backward_diff(field, axis_index):
    return field - jnp.roll(field, 1, axis_index)


def operate(velocity, shear_resistance_map):
    gradients = [[forward_diff(velocity[target], SPATIAL[source]) for source in range(3)] for target in range(3)]
    spread = gradients[0][0] + gradients[1][1] + gradients[2][2]
    result = []
    for target in range(3):
        summed = ANCHOR * velocity[target]
        for source in range(3):
            fluxes = shear_resistance_map * (gradients[target][source] + gradients[source][target])
            if target == source:
                fluxes = fluxes + AUGMENT * spread
            summed = summed - backward_diff(fluxes, SPATIAL[source])
        result.append(summed)
    return jnp.stack(result)


def pressure_gradient(pressure):
    return jnp.stack([-backward_diff(pressure, SPATIAL[target]) for target in range(3)])


def divergence(velocity):
    return forward_diff(velocity[0], SPATIAL[0]) + forward_diff(velocity[1], SPATIAL[1]) + forward_diff(velocity[2], SPATIAL[2])


def eigen_values(extent):
    index = jnp.arange(extent, dtype=jnp.int32).astype(jnp.float32)
    return 2.0 - 2.0 * jnp.cos((2.0 * jnp.pi / extent) * index)


def precondition(residual):
    ylength, zlength, period_extent_first = residual.shape[1], residual.shape[2], residual.shape[3]
    yeigen = eigen_values(ylength)
    zeigen = eigen_values(zlength)
    xeigen = eigen_values(period_extent_first)
    symbol = 1.0 / (SMOOTHING * (yeigen[:, None, None] + zeigen[None, :, None] + xeigen[None, None, :]) + ANCHOR)
    spectrum = jnp.fft.fftn(residual, axes=(1, 2, 3))
    return jnp.real(jnp.fft.ifftn(spectrum * symbol[None], axes=(1, 2, 3))).astype(residual.dtype)


def reference(prior_window_motion, prior_window_stress, heat_scalar):
    shear_resistance_map = jnp.exp(ENABLE_SWITCH * (1.0 / (heat_scalar + OFFSET_COUNT) - 1.0 / (0.5 + OFFSET_COUNT)))
    thermal_lift = RAYLEIGH_NUMBER * (heat_scalar - 0.5)
    zeroes = jnp.zeros_like(thermal_lift)
    forcing = jnp.stack([zeroes, zeroes, thermal_lift])
    velocity = prior_window_motion
    pressure = prior_window_stress
    for outer_step in range(OUTER):
        residual = forcing - pressure_gradient(pressure) - operate(velocity, shear_resistance_map)
        direction = residual
        energy_now = jnp.sum(residual * residual)
        for inner_step in range(INNER):
            precond = precondition(residual)
            energy_next = jnp.sum(residual * precond)
            if inner_step == 0:
                direction = precond
            else:
                direction = precond + (energy_next / energy_now) * direction
            energy_now = energy_next
            image = operate(direction, shear_resistance_map)
            step_size = energy_now / jnp.sum(direction * image)
            velocity = velocity + step_size * direction
            residual = residual - step_size * image
        pressure = pressure + AUGMENT * divergence(velocity)
    return velocity, pressure
```

```python
import jax
import jax.numpy as jnp
from jax import lax
from jax.sharding import PartitionSpec as P

OUTER = 2
INNER = 2


PRECISE = lax.Precision.HIGHEST
ENABLE_SWITCH = 2.0
OFFSET_COUNT = 0.5
AUGMENT = 1.0
ANCHOR = 0.002
RAYLEIGH_NUMBER = 1.0
SMOOTHING = 2.0


def padded(cells, sides, width):
    for axis, dim in sides:
        count = lax.axis_size(axis)
        head = lax.slice_in_dim(cells, 0, width, axis=dim)
        tail = lax.slice_in_dim(cells, cells.shape[dim] - width, cells.shape[dim], axis=dim)
        cells = jnp.concatenate(
            [
                lax.ppermute(tail, axis, [(i, (i + 1) % count) for i in range(count)]),
                cells,
                lax.ppermute(head, axis, [((i + 1) % count, i) for i in range(count)]),
            ],
            axis=dim,
        )
    return cells


def global_sum(value):
    count = lax.axis_size("row") * lax.axis_size("col")
    spread = jnp.broadcast_to(value.reshape(1), (count,))
    gathered = lax.all_to_all(spread, ("row", "col"), 0, 0, tiled=True)
    return jnp.sum(gathered)


def from_behind(value, axis, steps):
    count = lax.axis_size(axis)
    pairs = [(source, (source + steps) % count) for source in range(count)]
    return lax.ppermute(value, axis, pairs)


def cas_matrix(extent):
    index = jnp.arange(extent, dtype=jnp.int32)
    phase = index[:, None] * index[None, :] % extent
    angle = 2.0 * jnp.pi / extent * phase.astype(jnp.float32)
    return jnp.cos(angle) + jnp.sin(angle)


def eigen_row(number, offset_index, extent):
    index = offset_index + jnp.arange(number, dtype=jnp.int32)
    return 2.0 - 2.0 * jnp.cos(2.0 * jnp.pi / extent * index.astype(jnp.float32))


def precondition(residual, tables):
    xtable, ytable, ztable = tables
    row_count = lax.axis_size("row")
    col_count = lax.axis_size("col")
    components, owned_height_lines, owned_depth_slices, period_extent_first = residual.shape
    ylength = owned_height_lines * row_count
    zlength = owned_depth_slices * col_count
    normal_factor = 1.0 / (period_extent_first * ylength * zlength)
    xpiece = period_extent_first // row_count
    ypiece = ylength // col_count
    spectrum = jnp.einsum("kx,cyzx->cykz", xtable, residual, precision=PRECISE).reshape(
        components, owned_height_lines, period_extent_first * owned_depth_slices
    )
    spectrum = lax.all_to_all(spectrum, "row", split_axis=2, concat_axis=1, tiled=True)
    spectrum = jnp.einsum(
        "ky,cyxz->czkx",
        ytable,
        spectrum.reshape(components, ylength, xpiece, owned_depth_slices),
        precision=PRECISE,
    ).reshape(components, owned_depth_slices, ylength * xpiece)
    spectrum = lax.all_to_all(spectrum, "col", split_axis=2, concat_axis=1, tiled=True)
    zeigen = eigen_row(zlength, 0, zlength)
    yeigen = eigen_row(ypiece, lax.axis_index("col") * ypiece, ylength)
    xeigen = eigen_row(xpiece, lax.axis_index("row") * xpiece, period_extent_first)
    mixed_eigen = (yeigen[:, None] + xeigen[None, :]).reshape(-1)
    symbol = normal_factor / (SMOOTHING * (zeigen[:, None] + mixed_eigen[None, :]) + ANCHOR)
    spectrum = jnp.einsum("kz,czm->ckm", ztable, spectrum, precision=PRECISE)
    spectrum = jnp.einsum("kz,czm->ckm", ztable, spectrum * symbol[None], precision=PRECISE)
    spectrum = lax.all_to_all(spectrum, "col", split_axis=1, concat_axis=2, tiled=True)
    spectrum = jnp.einsum(
        "ky,czyx->ckxz",
        ytable,
        spectrum.reshape(components, owned_depth_slices, ylength, xpiece),
        precision=PRECISE,
    ).reshape(components, ylength, xpiece * owned_depth_slices)
    spectrum = lax.all_to_all(spectrum, "row", split_axis=1, concat_axis=2, tiled=True)
    return jnp.einsum(
        "kx,cyxz->cyzk",
        xtable,
        spectrum.reshape(components, owned_height_lines, period_extent_first, owned_depth_slices),
        precision=PRECISE,
    )


def forward(extended, direction):
    owned_height_lines = extended.shape[-3] - 2
    owned_depth_slices = extended.shape[-2] - 2
    root = extended[..., : owned_height_lines + 1, : owned_depth_slices + 1, :]
    if direction == 0:
        return jnp.roll(root, -1, -1) - root
    if direction == 1:
        return extended[..., 1 : owned_height_lines + 2, : owned_depth_slices + 1, :] - root
    return extended[..., : owned_height_lines + 1, 1 : owned_depth_slices + 2, :] - root


def backward(region, direction):
    center = region[..., 1:, 1:, :]
    if direction == 0:
        return center - jnp.roll(center, 1, -1)
    if direction == 1:
        return center - region[..., :-1, 1:, :]
    return center - region[..., 1:, :-1, :]


def extend(field):
    return padded(field, (("row", 1), ("col", 2)), 1)


def lower_region(pressure):
    below_y = from_behind(pressure[-1:], "row", 1)
    below_z = from_behind(pressure[:, -1:], "col", 1)
    corner = jnp.zeros((1, 1, pressure.shape[2]), jnp.float32)
    upper_band = jnp.concatenate([corner, below_y], 1)
    main_band = jnp.concatenate([below_z, pressure], 1)
    return jnp.concatenate([upper_band, main_band], 0)


def operate(extended, shear_resistance_map):
    owned_height_lines = extended.shape[1] - 2
    owned_depth_slices = extended.shape[2] - 2
    gradients = [[forward(extended[target], source) for source in range(3)] for target in range(3)]
    spread = gradients[0][0] + gradients[1][1] + gradients[2][2]
    result = []
    for target in range(3):
        summed = (
            ANCHOR * extended[target, 1 : owned_height_lines + 1, 1 : owned_depth_slices + 1, :]
        )
        for source in range(3):
            fluxes = shear_resistance_map * (gradients[target][source] + gradients[source][target])
            if target == source:
                fluxes = fluxes + AUGMENT * spread
            summed = summed - backward(fluxes, source)
        result.append(summed)
    return jnp.stack(result)


def pressure_gradient(region):
    return jnp.stack([-backward(region, target) for target in range(3)])


def divergence_region(extended):
    return forward(extended[0], 0) + forward(extended[1], 1) + forward(extended[2], 2)


def per_device(prior_window_motion, prior_window_stress, heat_scalar):
    owned_height_lines, owned_depth_slices, period_extent_first = heat_scalar.shape
    tables = (
        cas_matrix(period_extent_first),
        cas_matrix(owned_height_lines * lax.axis_size("row")),
        cas_matrix(owned_depth_slices * lax.axis_size("col")),
    )
    stacked_fields = jnp.concatenate(
        [prior_window_motion, prior_window_stress[None], heat_scalar[None]], 0
    )
    extended = padded(stacked_fields, (("row", 1), ("col", 2)), 1)
    shear_resistance_map = jnp.exp(
        ENABLE_SWITCH
        * (
            1.0
            / (extended[4, : owned_height_lines + 1, : owned_depth_slices + 1, :] + OFFSET_COUNT)
            - 1.0 / (0.5 + OFFSET_COUNT)
        )
    )
    thermal_lift = RAYLEIGH_NUMBER * (heat_scalar - 0.5)
    zeroes = jnp.zeros_like(thermal_lift)
    forcing = jnp.stack([zeroes, zeroes, thermal_lift])
    velocity = prior_window_motion
    pressure = prior_window_stress
    velocity_ext = extended[0:3]
    pushing = pressure_gradient(extended[3, : owned_height_lines + 1, : owned_depth_slices + 1, :])
    spread_now = jnp.zeros_like(shear_resistance_map)
    for outer_step in range(OUTER):
        if outer_step > 0:
            pushing = pressure_gradient(lower_region(pressure))
        residual = forcing - pushing - operate(velocity_ext, shear_resistance_map)
        direction = residual
        image = residual
        energy_now = jnp.float32(1.0)
        step_size = jnp.float32(1.0)
        for inner_step in range(INNER):
            precond = precondition(residual, tables)
            energy_next = global_sum(jnp.sum(residual * precond))
            if inner_step == 0:
                direction = precond
            else:
                direction = precond + energy_next / energy_now * direction
            energy_now = energy_next
            image = operate(extend(direction), shear_resistance_map)
            curvature = global_sum(jnp.sum(direction * image))
            step_size = energy_now / curvature
            velocity = velocity + step_size * direction
            residual = residual - step_size * image
        velocity_ext = extend(velocity)
        spread_now = divergence_region(velocity_ext)
        pressure = pressure + AUGMENT * spread_now[1:, 1:, :]
    return (velocity, pressure)


def solution(mesh):
    placed = (P(None, "row", "col", None), P("row", "col", None), P("row", "col", None))
    return jax.shard_map(
        per_device,
        mesh=mesh,
        in_specs=placed,
        out_specs=(P(None, "row", "col", None), P("row", "col", None)),
        check_vma=False,
    )
```

```python
import jax
import jax.numpy as jnp
from jax import lax
from jax.sharding import PartitionSpec as P

OUTER = 2
INNER = 2


PRECISE = lax.Precision.HIGHEST
ENABLE_SWITCH = 2.0
OFFSET_COUNT = 0.5
AUGMENT = 1.0
ANCHOR = 0.002
RAYLEIGH_NUMBER = 1.0
SMOOTHING = 2.0


def padded(cells, sides, width):
    for axis, dim in sides:
        count = lax.axis_size(axis)
        head = lax.slice_in_dim(cells, 0, width, axis=dim)
        tail = lax.slice_in_dim(cells, cells.shape[dim] - width, cells.shape[dim], axis=dim)
        cells = jnp.concatenate(
            [
                lax.ppermute(tail, axis, [(i, (i + 1) % count) for i in range(count)]),
                cells,
                lax.ppermute(head, axis, [((i + 1) % count, i) for i in range(count)]),
            ],
            axis=dim,
        )
    return cells


def global_sum(value):
    count = lax.axis_size("row") * lax.axis_size("col")
    spread = jnp.broadcast_to(value.reshape(1), (count,))
    gathered = lax.all_to_all(spread, ("row", "col"), 0, 0, tiled=True)
    return jnp.sum(gathered)


def from_behind(value, axis, steps):
    count = lax.axis_size(axis)
    pairs = [(source, (source + steps) % count) for source in range(count)]
    return lax.ppermute(value, axis, pairs)


def cas_matrix(extent):
    index = jnp.arange(extent, dtype=jnp.int32)
    phase = index[:, None] * index[None, :] % extent
    angle = 2.0 * jnp.pi / extent * phase.astype(jnp.float32)
    return jnp.cos(angle) + jnp.sin(angle)


def widened(table, pieces):
    extent = table.shape[0]
    width = extent // pieces
    index = jnp.arange(pieces * (width + 2), dtype=jnp.int32)
    rows = (index // (width + 2)) * width + index % (width + 2) - 1
    return table[rows % extent]


def eigen_row(number, offset_index, extent):
    index = offset_index + jnp.arange(number, dtype=jnp.int32)
    return 2.0 - 2.0 * jnp.cos(2.0 * jnp.pi / extent * index.astype(jnp.float32))


def precondition(residual, tables):
    xtable, ytable, ztable = tables
    row_count = lax.axis_size("row")
    col_count = lax.axis_size("col")
    components, owned_height_lines, owned_depth_slices, period_extent_first = residual.shape
    ylength = owned_height_lines * row_count
    zlength = owned_depth_slices * col_count
    normal_factor = 1.0 / (period_extent_first * ylength * zlength)
    xpiece = period_extent_first // row_count
    ypiece = ylength // col_count
    spectrum = jnp.einsum("kx,cyzx->cykz", xtable, residual, precision=PRECISE).reshape(
        components, owned_height_lines, period_extent_first * owned_depth_slices
    )
    spectrum = lax.all_to_all(spectrum, "row", split_axis=2, concat_axis=1, tiled=True)
    spectrum = jnp.einsum(
        "ky,cyxz->czkx",
        ytable,
        spectrum.reshape(components, ylength, xpiece, owned_depth_slices),
        precision=PRECISE,
    ).reshape(components, owned_depth_slices, ylength * xpiece)
    spectrum = lax.all_to_all(spectrum, "col", split_axis=2, concat_axis=1, tiled=True)
    zeigen = eigen_row(zlength, 0, zlength)
    yeigen = eigen_row(ypiece, lax.axis_index("col") * ypiece, ylength)
    xeigen = eigen_row(xpiece, lax.axis_index("row") * xpiece, period_extent_first)
    mixed_eigen = (yeigen[:, None] + xeigen[None, :]).reshape(-1)
    symbol = normal_factor / (SMOOTHING * (zeigen[:, None] + mixed_eigen[None, :]) + ANCHOR)
    spectrum = jnp.einsum("kz,czm->ckm", ztable, spectrum, precision=PRECISE)
    zwide = widened(ztable, col_count)
    ywide = widened(ytable, row_count)
    spectrum = jnp.einsum("kz,czm->ckm", zwide, spectrum * symbol[None], precision=PRECISE)
    spectrum = lax.all_to_all(spectrum, "col", split_axis=1, concat_axis=2, tiled=True)
    spectrum = jnp.einsum(
        "ky,czyx->ckxz",
        ywide,
        spectrum.reshape(components, owned_depth_slices + 2, ylength, xpiece),
        precision=PRECISE,
    ).reshape(components, row_count * (owned_height_lines + 2), xpiece * (owned_depth_slices + 2))
    spectrum = lax.all_to_all(spectrum, "row", split_axis=1, concat_axis=2, tiled=True)
    return jnp.einsum(
        "kx,cyxz->cyzk",
        xtable,
        spectrum.reshape(
            components, owned_height_lines + 2, period_extent_first, owned_depth_slices + 2
        ),
        precision=PRECISE,
    )


def forward(extended, direction):
    owned_height_lines = extended.shape[-3] - 2
    owned_depth_slices = extended.shape[-2] - 2
    root = extended[..., : owned_height_lines + 1, : owned_depth_slices + 1, :]
    if direction == 0:
        return jnp.roll(root, -1, -1) - root
    if direction == 1:
        return extended[..., 1 : owned_height_lines + 2, : owned_depth_slices + 1, :] - root
    return extended[..., : owned_height_lines + 1, 1 : owned_depth_slices + 2, :] - root


def backward(region, direction):
    center = region[..., 1:, 1:, :]
    if direction == 0:
        return center - jnp.roll(center, 1, -1)
    if direction == 1:
        return center - region[..., :-1, 1:, :]
    return center - region[..., 1:, :-1, :]


def extend(field):
    return padded(field, (("row", 1), ("col", 2)), 1)


def lower_region(pressure):
    below_y = from_behind(pressure[-1:], "row", 1)
    below_z = from_behind(pressure[:, -1:], "col", 1)
    corner = jnp.zeros((1, 1, pressure.shape[2]), jnp.float32)
    upper_band = jnp.concatenate([corner, below_y], 1)
    main_band = jnp.concatenate([below_z, pressure], 1)
    return jnp.concatenate([upper_band, main_band], 0)


def operate(extended, shear_resistance_map):
    owned_height_lines = extended.shape[1] - 2
    owned_depth_slices = extended.shape[2] - 2
    gradients = [[forward(extended[target], source) for source in range(3)] for target in range(3)]
    spread = gradients[0][0] + gradients[1][1] + gradients[2][2]
    result = []
    for target in range(3):
        summed = (
            ANCHOR * extended[target, 1 : owned_height_lines + 1, 1 : owned_depth_slices + 1, :]
        )
        for source in range(3):
            fluxes = shear_resistance_map * (gradients[target][source] + gradients[source][target])
            if target == source:
                fluxes = fluxes + AUGMENT * spread
            summed = summed - backward(fluxes, source)
        result.append(summed)
    return jnp.stack(result)


def pressure_gradient(region):
    return jnp.stack([-backward(region, target) for target in range(3)])


def divergence_region(extended):
    return forward(extended[0], 0) + forward(extended[1], 1) + forward(extended[2], 2)


def per_device(prior_window_motion, prior_window_stress, heat_scalar):
    owned_height_lines, owned_depth_slices, period_extent_first = heat_scalar.shape
    tables = (
        cas_matrix(period_extent_first),
        cas_matrix(owned_height_lines * lax.axis_size("row")),
        cas_matrix(owned_depth_slices * lax.axis_size("col")),
    )
    stacked_fields = jnp.concatenate(
        [prior_window_motion, prior_window_stress[None], heat_scalar[None]], 0
    )
    extended = padded(stacked_fields, (("row", 1), ("col", 2)), 1)
    shear_resistance_map = jnp.exp(
        ENABLE_SWITCH
        * (
            1.0
            / (extended[4, : owned_height_lines + 1, : owned_depth_slices + 1, :] + OFFSET_COUNT)
            - 1.0 / (0.5 + OFFSET_COUNT)
        )
    )
    thermal_lift = RAYLEIGH_NUMBER * (heat_scalar - 0.5)
    zeroes = jnp.zeros_like(thermal_lift)
    forcing = jnp.stack([zeroes, zeroes, thermal_lift])
    velocity_ext = extended[0:3]
    pressure_low = extended[3, : owned_height_lines + 1, : owned_depth_slices + 1, :]
    for outer_step in range(OUTER):
        pushing = pressure_gradient(pressure_low)
        residual = forcing - pushing - operate(velocity_ext, shear_resistance_map)
        direction_ext = None
        energy_now = jnp.float32(1.0)
        for inner_step in range(INNER):
            precond_ext = precondition(residual, tables)
            precond = precond_ext[:, 1 : owned_height_lines + 1, 1 : owned_depth_slices + 1, :]
            energy_next = global_sum(jnp.sum(residual * precond))
            if inner_step == 0:
                direction_ext = precond_ext
            else:
                direction_ext = precond_ext + energy_next / energy_now * direction_ext
            energy_now = energy_next
            direction = direction_ext[:, 1 : owned_height_lines + 1, 1 : owned_depth_slices + 1, :]
            image = operate(direction_ext, shear_resistance_map)
            curvature = global_sum(jnp.sum(direction * image))
            step_size = energy_now / curvature
            velocity_ext = velocity_ext + step_size * direction_ext
            residual = residual - step_size * image
        spread_now = divergence_region(velocity_ext)
        pressure_low = pressure_low + AUGMENT * spread_now
    velocity = velocity_ext[:, 1 : owned_height_lines + 1, 1 : owned_depth_slices + 1, :]
    pressure = pressure_low[1:, 1:, :]
    return (velocity, pressure)


def solution(mesh):
    placed = (P(None, "row", "col", None), P("row", "col", None), P("row", "col", None))
    return jax.shard_map(
        per_device,
        mesh=mesh,
        in_specs=placed,
        out_specs=(P(None, "row", "col", None), P("row", "col", None)),
        check_vma=False,
    )
```

```python
import jax
import jax.numpy as jnp
from jax import lax
from jax.sharding import PartitionSpec as P

OUTER = 2
INNER = 2


PRECISE = lax.Precision.HIGHEST
ENABLE_SWITCH = 2.0
OFFSET_COUNT = 0.5
AUGMENT = 1.0
ANCHOR = 0.002
RAYLEIGH_NUMBER = 1.0
SMOOTHING = 2.0


def padded(cells, sides, width):
    for axis, dim in sides:
        count = lax.axis_size(axis)
        head = lax.slice_in_dim(cells, 0, width, axis=dim)
        tail = lax.slice_in_dim(cells, cells.shape[dim] - width, cells.shape[dim], axis=dim)
        cells = jnp.concatenate(
            [
                lax.ppermute(tail, axis, [(i, (i + 1) % count) for i in range(count)]),
                cells,
                lax.ppermute(head, axis, [((i + 1) % count, i) for i in range(count)]),
            ],
            axis=dim,
        )
    return cells


def global_sum(value):
    count = lax.axis_size("row") * lax.axis_size("col")
    spread = jnp.broadcast_to(value.reshape(1), (count,))
    gathered = lax.all_to_all(spread, ("row", "col"), 0, 0, tiled=True)
    return jnp.sum(gathered)


def from_behind(value, axis, steps):
    count = lax.axis_size(axis)
    pairs = [(source, (source + steps) % count) for source in range(count)]
    return lax.ppermute(value, axis, pairs)


def cas_matrix(extent):
    index = jnp.arange(extent, dtype=jnp.int32)
    phase = index[:, None] * index[None, :] % extent
    angle = 2.0 * jnp.pi / extent * phase.astype(jnp.float32)
    return jnp.cos(angle) + jnp.sin(angle)


def widened(table, pieces):
    extent = table.shape[0]
    width = extent // pieces
    index = jnp.arange(pieces * (width + 2), dtype=jnp.int32)
    rows = (index // (width + 2)) * width + index % (width + 2) - 1
    return table[rows % extent]


def eigen_row(number, offset_index, extent):
    index = offset_index + jnp.arange(number, dtype=jnp.int32)
    return 2.0 - 2.0 * jnp.cos(2.0 * jnp.pi / extent * index.astype(jnp.float32))


def exchange(cells, partial, axis, split_axis, concat_axis):
    count = lax.axis_size(axis)
    rider = jnp.broadcast_to(partial.astype(cells.dtype), (1,) + cells.shape[1:])
    moved = lax.all_to_all(
        jnp.concatenate([cells, rider], 0), axis, split_axis, concat_axis, tiled=True
    )
    arrived = jnp.moveaxis(moved[-1], concat_axis - 1, 0)
    arrived = arrived.reshape(count, arrived.shape[0] // count, -1)[:, 0, 0]
    return moved[:-1], jnp.sum(arrived)


def spectral_symbol(shape):
    row_count = lax.axis_size("row")
    col_count = lax.axis_size("col")
    components, owned_height_lines, owned_depth_slices, period_extent_first = shape
    ylength = owned_height_lines * row_count
    zlength = owned_depth_slices * col_count
    normal_factor = 1.0 / (period_extent_first * ylength * zlength)
    xpiece = period_extent_first // row_count
    ypiece = ylength // col_count
    zeigen = eigen_row(zlength, 0, zlength)
    yeigen = eigen_row(ypiece, lax.axis_index("col") * ypiece, ylength)
    xeigen = eigen_row(xpiece, lax.axis_index("row") * xpiece, period_extent_first)
    mixed_eigen = (yeigen[:, None] + xeigen[None, :]).reshape(-1)
    return normal_factor / (SMOOTHING * (zeigen[:, None] + mixed_eigen[None, :]) + ANCHOR)


def transform_forward(residual, tables, partial):
    xtable, ytable, ztable = tables
    row_count = lax.axis_size("row")
    components, owned_height_lines, owned_depth_slices, period_extent_first = residual.shape
    ylength = owned_height_lines * row_count
    xpiece = period_extent_first // row_count
    spectrum = jnp.einsum("kx,cyzx->cykz", xtable, residual, precision=PRECISE).reshape(
        components, owned_height_lines, period_extent_first * owned_depth_slices
    )
    spectrum, partial = exchange(spectrum, partial, "row", 2, 1)
    spectrum = jnp.einsum(
        "ky,cyxz->czkx",
        ytable,
        spectrum.reshape(components, ylength, xpiece, owned_depth_slices),
        precision=PRECISE,
    ).reshape(components, owned_depth_slices, ylength * xpiece)
    spectrum, partial = exchange(spectrum, partial, "col", 2, 1)
    return jnp.einsum("kz,czm->ckm", ztable, spectrum, precision=PRECISE), partial


def transform_inverse(filtered, tables, partial, shape):
    xtable, ytable, ztable = tables
    row_count = lax.axis_size("row")
    col_count = lax.axis_size("col")
    components, owned_height_lines, owned_depth_slices, period_extent_first = shape
    ylength = owned_height_lines * row_count
    xpiece = period_extent_first // row_count
    zwide = widened(ztable, col_count)
    ywide = widened(ytable, row_count)
    spectrum = jnp.einsum("kz,czm->ckm", zwide, filtered, precision=PRECISE)
    spectrum, partial = exchange(spectrum, partial, "col", 1, 2)
    spectrum = jnp.einsum(
        "ky,czyx->ckxz",
        ywide,
        spectrum.reshape(components, owned_depth_slices + 2, ylength, xpiece),
        precision=PRECISE,
    ).reshape(components, row_count * (owned_height_lines + 2), xpiece * (owned_depth_slices + 2))
    spectrum, partial = exchange(spectrum, partial, "row", 1, 2)
    return jnp.einsum(
        "kx,cyxz->cyzk",
        xtable,
        spectrum.reshape(
            components, owned_height_lines + 2, period_extent_first, owned_depth_slices + 2
        ),
        precision=PRECISE,
    ), partial


def forward(extended, direction):
    owned_height_lines = extended.shape[-3] - 2
    owned_depth_slices = extended.shape[-2] - 2
    root = extended[..., : owned_height_lines + 1, : owned_depth_slices + 1, :]
    if direction == 0:
        return jnp.roll(root, -1, -1) - root
    if direction == 1:
        return extended[..., 1 : owned_height_lines + 2, : owned_depth_slices + 1, :] - root
    return extended[..., : owned_height_lines + 1, 1 : owned_depth_slices + 2, :] - root


def backward(region, direction):
    center = region[..., 1:, 1:, :]
    if direction == 0:
        return center - jnp.roll(center, 1, -1)
    if direction == 1:
        return center - region[..., :-1, 1:, :]
    return center - region[..., 1:, :-1, :]


def extend(field):
    return padded(field, (("row", 1), ("col", 2)), 1)


def lower_region(pressure):
    below_y = from_behind(pressure[-1:], "row", 1)
    below_z = from_behind(pressure[:, -1:], "col", 1)
    corner = jnp.zeros((1, 1, pressure.shape[2]), jnp.float32)
    upper_band = jnp.concatenate([corner, below_y], 1)
    main_band = jnp.concatenate([below_z, pressure], 1)
    return jnp.concatenate([upper_band, main_band], 0)


def operate(extended, shear_resistance_map):
    owned_height_lines = extended.shape[1] - 2
    owned_depth_slices = extended.shape[2] - 2
    gradients = [[forward(extended[target], source) for source in range(3)] for target in range(3)]
    spread = gradients[0][0] + gradients[1][1] + gradients[2][2]
    result = []
    for target in range(3):
        summed = (
            ANCHOR * extended[target, 1 : owned_height_lines + 1, 1 : owned_depth_slices + 1, :]
        )
        for source in range(3):
            fluxes = shear_resistance_map * (gradients[target][source] + gradients[source][target])
            if target == source:
                fluxes = fluxes + AUGMENT * spread
            summed = summed - backward(fluxes, source)
        result.append(summed)
    return jnp.stack(result)


def pressure_gradient(region):
    return jnp.stack([-backward(region, target) for target in range(3)])


def divergence_region(extended):
    return forward(extended[0], 0) + forward(extended[1], 1) + forward(extended[2], 2)


def per_device(prior_window_motion, prior_window_stress, heat_scalar):
    owned_height_lines, owned_depth_slices, period_extent_first = heat_scalar.shape
    tables = (
        cas_matrix(period_extent_first),
        cas_matrix(owned_height_lines * lax.axis_size("row")),
        cas_matrix(owned_depth_slices * lax.axis_size("col")),
    )
    stacked_fields = jnp.concatenate(
        [prior_window_motion, prior_window_stress[None], heat_scalar[None]], 0
    )
    extended = padded(stacked_fields, (("row", 1), ("col", 2)), 1)
    shear_resistance_map = jnp.exp(
        ENABLE_SWITCH
        * (
            1.0
            / (extended[4, : owned_height_lines + 1, : owned_depth_slices + 1, :] + OFFSET_COUNT)
            - 1.0 / (0.5 + OFFSET_COUNT)
        )
    )
    thermal_lift = RAYLEIGH_NUMBER * (heat_scalar - 0.5)
    zeroes = jnp.zeros_like(thermal_lift)
    forcing = jnp.stack([zeroes, zeroes, thermal_lift])
    velocity_ext = extended[0:3]
    pressure_low = extended[3, : owned_height_lines + 1, : owned_depth_slices + 1, :]
    symbol = spectral_symbol(prior_window_motion.shape)
    inner_cells = (slice(None), slice(1, owned_height_lines + 1), slice(1, owned_depth_slices + 1))
    for outer_step in range(OUTER):
        pushing = pressure_gradient(pressure_low)
        residual = forcing - pushing - operate(velocity_ext, shear_resistance_map)
        spectrum, _ = transform_forward(residual, tables, jnp.float32(0.0))
        direction_ext = None
        energy_now = jnp.float32(1.0)
        for inner_step in range(INNER):
            if inner_step > 0:
                image_spectrum, curvature = transform_forward(image, tables, curvature_part)
                step_size = energy_now / curvature
                velocity_ext = velocity_ext + step_size * direction_ext
                spectrum = spectrum - step_size * image_spectrum
            filtered = spectrum * symbol[None]
            precond_ext, energy_next = transform_inverse(
                filtered, tables, jnp.sum(spectrum * filtered), prior_window_motion.shape
            )
            if inner_step == 0:
                direction_ext = precond_ext
            else:
                direction_ext = precond_ext + energy_next / energy_now * direction_ext
            energy_now = energy_next
            image = operate(direction_ext, shear_resistance_map)
            curvature_part = jnp.sum(direction_ext[inner_cells] * image)
        step_size = energy_now / global_sum(curvature_part)
        velocity_ext = velocity_ext + step_size * direction_ext
        spread_now = divergence_region(velocity_ext)
        pressure_low = pressure_low + AUGMENT * spread_now
    velocity = velocity_ext[:, 1 : owned_height_lines + 1, 1 : owned_depth_slices + 1, :]
    pressure = pressure_low[1:, 1:, :]
    return (velocity, pressure)


def solution(mesh):
    placed = (P(None, "row", "col", None), P("row", "col", None), P("row", "col", None))
    return jax.shard_map(
        per_device,
        mesh=mesh,
        in_specs=placed,
        out_specs=(P(None, "row", "col", None), P("row", "col", None)),
        check_vma=False,
    )
```

```python
import jax
import jax.numpy as jnp
from jax import lax
from jax.sharding import PartitionSpec as P

OUTER = 2
INNER = 2


PRECISE = lax.Precision.HIGHEST
ENABLE_SWITCH = 2.0
OFFSET_COUNT = 0.5
AUGMENT = 1.0
ANCHOR = 0.002
RAYLEIGH_NUMBER = 1.0
SMOOTHING = 2.0


def padded(cells, sides, width):
    for axis, dim in sides:
        count = lax.axis_size(axis)
        head = lax.slice_in_dim(cells, 0, width, axis=dim)
        tail = lax.slice_in_dim(cells, cells.shape[dim] - width, cells.shape[dim], axis=dim)
        cells = jnp.concatenate(
            [
                lax.ppermute(tail, axis, [(i, (i + 1) % count) for i in range(count)]),
                cells,
                lax.ppermute(head, axis, [((i + 1) % count, i) for i in range(count)]),
            ],
            axis=dim,
        )
    return cells


def global_sum(value):
    count = lax.axis_size("row") * lax.axis_size("col")
    spread = jnp.broadcast_to(value.reshape(1), (count,))
    gathered = lax.all_to_all(spread, ("row", "col"), 0, 0, tiled=True)
    return jnp.sum(gathered)


def from_behind(value, axis, steps):
    count = lax.axis_size(axis)
    pairs = [(source, (source + steps) % count) for source in range(count)]
    return lax.ppermute(value, axis, pairs)


def cas_matrix(extent):
    index = jnp.arange(extent, dtype=jnp.int32)
    phase = index[:, None] * index[None, :] % extent
    angle = 2.0 * jnp.pi / extent * phase.astype(jnp.float32)
    return jnp.cos(angle) + jnp.sin(angle)


def widened(table, pieces):
    extent = table.shape[0]
    width = extent // pieces
    index = jnp.arange(pieces * (width + 2), dtype=jnp.int32)
    rows = (index // (width + 2)) * width + index % (width + 2) - 1
    return table[rows % extent]


def eigen_row(number, offset_index, extent):
    index = offset_index + jnp.arange(number, dtype=jnp.int32)
    return 2.0 - 2.0 * jnp.cos(2.0 * jnp.pi / extent * index.astype(jnp.float32))


def exchange(cells, partial, axis, split_axis, concat_axis):
    if partial is None:
        moved = lax.all_to_all(cells, axis, split_axis, concat_axis, tiled=True)
        return moved, None
    count = lax.axis_size(axis)
    rider = jnp.broadcast_to(partial.astype(cells.dtype), (1,) + cells.shape[1:])
    moved = lax.all_to_all(
        jnp.concatenate([cells, rider], 0), axis, split_axis, concat_axis, tiled=True
    )
    arrived = jnp.moveaxis(moved[-1], concat_axis - 1, 0)
    arrived = arrived.reshape(count, arrived.shape[0] // count, -1)[:, 0, 0]
    return moved[:-1], jnp.sum(arrived)


def spectral_symbol(shape):
    row_count = lax.axis_size("row")
    col_count = lax.axis_size("col")
    components, owned_height_lines, owned_depth_slices, period_extent_first = shape
    ylength = owned_height_lines * row_count
    zlength = owned_depth_slices * col_count
    normal_factor = 1.0 / (period_extent_first * ylength * zlength)
    xpiece = period_extent_first // row_count
    ypiece = ylength // col_count
    zeigen = eigen_row(zlength, 0, zlength)
    yeigen = eigen_row(ypiece, lax.axis_index("col") * ypiece, ylength)
    xeigen = eigen_row(xpiece, lax.axis_index("row") * xpiece, period_extent_first)
    mixed_eigen = (yeigen[:, None] + xeigen[None, :]).reshape(-1)
    return normal_factor / (SMOOTHING * (zeigen[:, None] + mixed_eigen[None, :]) + ANCHOR)


def transform_forward(residual, tables, partial):
    xtable, ytable, ztable = tables
    row_count = lax.axis_size("row")
    components, owned_height_lines, owned_depth_slices, period_extent_first = residual.shape
    ylength = owned_height_lines * row_count
    xpiece = period_extent_first // row_count
    spectrum = jnp.einsum("kx,cyzx->cykz", xtable, residual, precision=PRECISE).reshape(
        components, owned_height_lines, period_extent_first * owned_depth_slices
    )
    spectrum, partial = exchange(spectrum, partial, "row", 2, 1)
    spectrum = jnp.einsum(
        "ky,cyxz->czkx",
        ytable,
        spectrum.reshape(components, ylength, xpiece, owned_depth_slices),
        precision=PRECISE,
    ).reshape(components, owned_depth_slices, ylength * xpiece)
    spectrum, partial = exchange(spectrum, partial, "col", 2, 1)
    return jnp.einsum("kz,czm->ckm", ztable, spectrum, precision=PRECISE), partial


def transform_inverse(filtered, tables, partial, shape):
    xtable, ytable, ztable = tables
    row_count = lax.axis_size("row")
    col_count = lax.axis_size("col")
    components, owned_height_lines, owned_depth_slices, period_extent_first = shape
    ylength = owned_height_lines * row_count
    xpiece = period_extent_first // row_count
    zwide = widened(ztable, col_count)
    ywide = widened(ytable, row_count)
    spectrum = jnp.einsum("kz,czm->ckm", zwide, filtered, precision=PRECISE)
    spectrum, partial = exchange(spectrum, partial, "col", 1, 2)
    spectrum = jnp.einsum(
        "ky,czyx->ckxz",
        ywide,
        spectrum.reshape(components, owned_depth_slices + 2, ylength, xpiece),
        precision=PRECISE,
    ).reshape(components, row_count * (owned_height_lines + 2), xpiece * (owned_depth_slices + 2))
    spectrum, partial = exchange(spectrum, partial, "row", 1, 2)
    return jnp.einsum(
        "kx,cyxz->cyzk",
        xtable,
        spectrum.reshape(
            components, owned_height_lines + 2, period_extent_first, owned_depth_slices + 2
        ),
        precision=PRECISE,
    ), partial


def forward(extended, direction):
    owned_height_lines = extended.shape[-3] - 2
    owned_depth_slices = extended.shape[-2] - 2
    root = extended[..., : owned_height_lines + 1, : owned_depth_slices + 1, :]
    if direction == 0:
        return jnp.roll(root, -1, -1) - root
    if direction == 1:
        return extended[..., 1 : owned_height_lines + 2, : owned_depth_slices + 1, :] - root
    return extended[..., : owned_height_lines + 1, 1 : owned_depth_slices + 2, :] - root


def backward(region, direction):
    center = region[..., 1:, 1:, :]
    if direction == 0:
        return center - jnp.roll(center, 1, -1)
    if direction == 1:
        return center - region[..., :-1, 1:, :]
    return center - region[..., 1:, :-1, :]


def extend(field):
    return padded(field, (("row", 1), ("col", 2)), 1)


def lower_region(pressure):
    below_y = from_behind(pressure[-1:], "row", 1)
    below_z = from_behind(pressure[:, -1:], "col", 1)
    corner = jnp.zeros((1, 1, pressure.shape[2]), jnp.float32)
    upper_band = jnp.concatenate([corner, below_y], 1)
    main_band = jnp.concatenate([below_z, pressure], 1)
    return jnp.concatenate([upper_band, main_band], 0)


def operate(extended, shear_resistance_map):
    owned_height_lines = extended.shape[1] - 2
    owned_depth_slices = extended.shape[2] - 2
    gradients = [[forward(extended[target], source) for source in range(3)] for target in range(3)]
    spread = gradients[0][0] + gradients[1][1] + gradients[2][2]
    result = []
    for target in range(3):
        summed = (
            ANCHOR * extended[target, 1 : owned_height_lines + 1, 1 : owned_depth_slices + 1, :]
        )
        for source in range(3):
            fluxes = shear_resistance_map * (gradients[target][source] + gradients[source][target])
            if target == source:
                fluxes = fluxes + AUGMENT * spread
            summed = summed - backward(fluxes, source)
        result.append(summed)
    return jnp.stack(result)


def pressure_gradient(region):
    return jnp.stack([-backward(region, target) for target in range(3)])


def divergence_region(extended):
    return forward(extended[0], 0) + forward(extended[1], 1) + forward(extended[2], 2)


def per_device(prior_window_motion, prior_window_stress, heat_scalar):
    owned_height_lines, owned_depth_slices, period_extent_first = heat_scalar.shape
    tables = (
        cas_matrix(period_extent_first),
        cas_matrix(owned_height_lines * lax.axis_size("row")),
        cas_matrix(owned_depth_slices * lax.axis_size("col")),
    )
    stacked_fields = jnp.concatenate(
        [prior_window_motion, prior_window_stress[None], heat_scalar[None]], 0
    )
    extended = padded(stacked_fields, (("row", 1), ("col", 2)), 1)
    shear_resistance_map = jnp.exp(
        ENABLE_SWITCH
        * (
            1.0
            / (extended[4, : owned_height_lines + 1, : owned_depth_slices + 1, :] + OFFSET_COUNT)
            - 1.0 / (0.5 + OFFSET_COUNT)
        )
    )
    thermal_lift = RAYLEIGH_NUMBER * (heat_scalar - 0.5)
    zeroes = jnp.zeros_like(thermal_lift)
    forcing = jnp.stack([zeroes, zeroes, thermal_lift])
    velocity_ext = extended[0:3]
    pressure_low = extended[3, : owned_height_lines + 1, : owned_depth_slices + 1, :]
    symbol = spectral_symbol(prior_window_motion.shape)
    inner_cells = (slice(None), slice(1, owned_height_lines + 1), slice(1, owned_depth_slices + 1))
    for outer_step in range(OUTER):
        pushing = pressure_gradient(pressure_low)
        residual = forcing - pushing - operate(velocity_ext, shear_resistance_map)
        spectrum, _ = transform_forward(residual, tables, None)
        direction_ext = None
        energy_now = jnp.float32(1.0)
        for inner_step in range(INNER):
            if inner_step > 0:
                image_spectrum, curvature = transform_forward(image, tables, curvature_part)
                step_size = energy_now / curvature
                velocity_ext = velocity_ext + step_size * direction_ext
                spectrum = spectrum - step_size * image_spectrum
            filtered = spectrum * symbol[None]
            precond_ext, energy_next = transform_inverse(
                filtered, tables, jnp.sum(spectrum * filtered), prior_window_motion.shape
            )
            if inner_step == 0:
                direction_ext = precond_ext
            else:
                direction_ext = precond_ext + energy_next / energy_now * direction_ext
            energy_now = energy_next
            image = operate(direction_ext, shear_resistance_map)
            curvature_part = jnp.sum(direction_ext[inner_cells] * image)
        step_size = energy_now / global_sum(curvature_part)
        velocity_ext = velocity_ext + step_size * direction_ext
        spread_now = divergence_region(velocity_ext)
        pressure_low = pressure_low + AUGMENT * spread_now
    velocity = velocity_ext[:, 1 : owned_height_lines + 1, 1 : owned_depth_slices + 1, :]
    pressure = pressure_low[1:, 1:, :]
    return (velocity, pressure)


def solution(mesh):
    placed = (P(None, "row", "col", None), P("row", "col", None), P("row", "col", None))
    return jax.shard_map(
        per_device,
        mesh=mesh,
        in_specs=placed,
        out_specs=(P(None, "row", "col", None), P("row", "col", None)),
        check_vma=False,
    )
```

```python
import jax
import jax.numpy as jnp
from jax import lax
from jax.sharding import PartitionSpec as P

OUTER = 2
INNER = 2


PRECISE = lax.Precision.HIGHEST
ENABLE_SWITCH = 2.0
OFFSET_COUNT = 0.5
AUGMENT = 1.0
ANCHOR = 0.002
RAYLEIGH_NUMBER = 1.0
SMOOTHING = 2.0


def padded(cells, sides, width):
    for axis, dim in sides:
        count = lax.axis_size(axis)
        head = lax.slice_in_dim(cells, 0, width, axis=dim)
        tail = lax.slice_in_dim(cells, cells.shape[dim] - width, cells.shape[dim], axis=dim)
        cells = jnp.concatenate(
            [
                lax.ppermute(tail, axis, [(i, (i + 1) % count) for i in range(count)]),
                cells,
                lax.ppermute(head, axis, [((i + 1) % count, i) for i in range(count)]),
            ],
            axis=dim,
        )
    return cells


def global_sum(value):
    count = lax.axis_size("row") * lax.axis_size("col")
    spread = jnp.broadcast_to(value.reshape(1), (count,))
    gathered = lax.all_to_all(spread, ("row", "col"), 0, 0, tiled=True)
    return jnp.sum(gathered)


def from_behind(value, axis, steps):
    count = lax.axis_size(axis)
    pairs = [(source, (source + steps) % count) for source in range(count)]
    return lax.ppermute(value, axis, pairs)


def cas_matrix(extent):
    index = jnp.arange(extent, dtype=jnp.int32)
    phase = index[:, None] * index[None, :] % extent
    angle = 2.0 * jnp.pi / extent * phase.astype(jnp.float32)
    return jnp.cos(angle) + jnp.sin(angle)


def widened(table, pieces):
    extent = table.shape[0]
    width = extent // pieces
    index = jnp.arange(pieces * (width + 2), dtype=jnp.int32)
    rows = (index // (width + 2)) * width + index % (width + 2) - 1
    return table[rows % extent]


def eigen_row(number, offset_index, extent):
    index = offset_index + jnp.arange(number, dtype=jnp.int32)
    return 2.0 - 2.0 * jnp.cos(2.0 * jnp.pi / extent * index.astype(jnp.float32))


def exchange(cells, partial, axis, split_axis, concat_axis):
    if partial is None:
        moved = lax.all_to_all(cells, axis, split_axis, concat_axis, tiled=True)
        return moved, None
    count = lax.axis_size(axis)
    rider = jnp.broadcast_to(partial.astype(cells.dtype), (1,) + cells.shape[1:])
    moved = lax.all_to_all(
        jnp.concatenate([cells, rider], 0), axis, split_axis, concat_axis, tiled=True
    )
    arrived = jnp.moveaxis(moved[-1], concat_axis - 1, 0)
    arrived = arrived.reshape(count, arrived.shape[0] // count, -1)[:, 0, 0]
    return moved[:-1], jnp.sum(arrived)


def spectral_symbol(shape):
    row_count = lax.axis_size("row")
    col_count = lax.axis_size("col")
    components, owned_height_lines, owned_depth_slices, period_extent_first = shape
    ylength = owned_height_lines * row_count
    zlength = owned_depth_slices * col_count
    normal_factor = 1.0 / (period_extent_first * ylength * zlength)
    xpiece = period_extent_first // row_count
    ypiece = ylength // col_count
    zeigen = eigen_row(zlength, 0, zlength)
    yeigen = eigen_row(ypiece, lax.axis_index("col") * ypiece, ylength)
    xeigen = eigen_row(xpiece, lax.axis_index("row") * xpiece, period_extent_first)
    mixed_eigen = (yeigen[:, None] + xeigen[None, :]).reshape(-1)
    return normal_factor / (SMOOTHING * (zeigen[:, None] + mixed_eigen[None, :]) + ANCHOR)


def transform_forward(residual, tables, partial):
    xtable, ytable, ztable = tables
    row_count = lax.axis_size("row")
    components, owned_height_lines, owned_depth_slices, period_extent_first = residual.shape
    ylength = owned_height_lines * row_count
    xpiece = period_extent_first // row_count
    spectrum = jnp.einsum("kx,cyzx->cykz", xtable, residual, precision=PRECISE).reshape(
        components, owned_height_lines, period_extent_first * owned_depth_slices
    )
    spectrum, partial = exchange(spectrum, partial, "row", 2, 1)
    spectrum = jnp.einsum(
        "ky,cyxz->czkx",
        ytable,
        spectrum.reshape(components, ylength, xpiece, owned_depth_slices),
        precision=PRECISE,
    ).reshape(components, owned_depth_slices, ylength * xpiece)
    spectrum, partial = exchange(spectrum, partial, "col", 2, 1)
    return jnp.einsum("kz,czm->ckm", ztable, spectrum, precision=PRECISE), partial


def transform_inverse(filtered, tables, partial, shape):
    xtable, ytable, ztable = tables
    row_count = lax.axis_size("row")
    col_count = lax.axis_size("col")
    components, owned_height_lines, owned_depth_slices, period_extent_first = shape
    ylength = owned_height_lines * row_count
    xpiece = period_extent_first // row_count
    zwide = widened(ztable, col_count)
    ywide = widened(ytable, row_count)
    spectrum = jnp.einsum("kz,czm->ckm", zwide, filtered, precision=PRECISE)
    spectrum, partial = exchange(spectrum, partial, "col", 1, 2)
    spectrum = jnp.einsum(
        "ky,czyx->ckxz",
        ywide,
        spectrum.reshape(components, owned_depth_slices + 2, ylength, xpiece),
        precision=PRECISE,
    ).reshape(components, row_count * (owned_height_lines + 2), xpiece * (owned_depth_slices + 2))
    spectrum, partial = exchange(spectrum, partial, "row", 1, 2)
    return jnp.einsum(
        "kx,cyxz->cyzk",
        xtable,
        spectrum.reshape(
            components, owned_height_lines + 2, period_extent_first, owned_depth_slices + 2
        ),
        precision=PRECISE,
    ), partial


def forward(extended, direction):
    owned_height_lines = extended.shape[-3] - 2
    owned_depth_slices = extended.shape[-2] - 2
    root = extended[..., : owned_height_lines + 1, : owned_depth_slices + 1, :]
    if direction == 0:
        return jnp.roll(root, -1, -1) - root
    if direction == 1:
        return extended[..., 1 : owned_height_lines + 2, : owned_depth_slices + 1, :] - root
    return extended[..., : owned_height_lines + 1, 1 : owned_depth_slices + 2, :] - root


def backward(region, direction):
    center = region[..., 1:, 1:, :]
    if direction == 0:
        return center - jnp.roll(center, 1, -1)
    if direction == 1:
        return center - region[..., :-1, 1:, :]
    return center - region[..., 1:, :-1, :]


def extend(field):
    return padded(field, (("row", 1), ("col", 2)), 1)


def lower_region(pressure):
    below_y = from_behind(pressure[-1:], "row", 1)
    below_z = from_behind(pressure[:, -1:], "col", 1)
    corner = jnp.zeros((1, 1, pressure.shape[2]), jnp.float32)
    upper_band = jnp.concatenate([corner, below_y], 1)
    main_band = jnp.concatenate([below_z, pressure], 1)
    return jnp.concatenate([upper_band, main_band], 0)


def operate(extended, shear_resistance_map):
    owned_height_lines = extended.shape[1] - 2
    owned_depth_slices = extended.shape[2] - 2
    gradients = [[forward(extended[target], source) for source in range(3)] for target in range(3)]
    spread = gradients[0][0] + gradients[1][1] + gradients[2][2]
    result = []
    for target in range(3):
        summed = (
            ANCHOR * extended[target, 1 : owned_height_lines + 1, 1 : owned_depth_slices + 1, :]
        )
        for source in range(3):
            fluxes = shear_resistance_map * (gradients[target][source] + gradients[source][target])
            if target == source:
                fluxes = fluxes + AUGMENT * spread
            summed = summed - backward(fluxes, source)
        result.append(summed)
    return jnp.stack(result)


def pressure_gradient(region):
    return jnp.stack([-backward(region, target) for target in range(3)])


def divergence_region(extended):
    return forward(extended[0], 0) + forward(extended[1], 1) + forward(extended[2], 2)


def per_device(prior_window_motion, prior_window_stress, heat_scalar):
    owned_height_lines, owned_depth_slices, period_extent_first = heat_scalar.shape
    tables = (
        cas_matrix(period_extent_first),
        cas_matrix(owned_height_lines * lax.axis_size("row")),
        cas_matrix(owned_depth_slices * lax.axis_size("col")),
    )
    stacked_fields = jnp.concatenate(
        [prior_window_motion, prior_window_stress[None], heat_scalar[None]], 0
    )
    extended = padded(stacked_fields, (("row", 1), ("col", 2)), 1)
    shear_resistance_map = jnp.exp(
        ENABLE_SWITCH
        * (
            1.0
            / (extended[4, : owned_height_lines + 1, : owned_depth_slices + 1, :] + OFFSET_COUNT)
            - 1.0 / (0.5 + OFFSET_COUNT)
        )
    )
    thermal_lift = RAYLEIGH_NUMBER * (heat_scalar - 0.5)
    zeroes = jnp.zeros_like(thermal_lift)
    forcing = jnp.stack([zeroes, zeroes, thermal_lift])
    velocity_ext = extended[0:3]
    pressure_low = extended[3, : owned_height_lines + 1, : owned_depth_slices + 1, :]
    symbol = spectral_symbol(prior_window_motion.shape)
    inner_cells = (slice(None), slice(1, owned_height_lines + 1), slice(1, owned_depth_slices + 1))
    pushing = pressure_gradient(pressure_low)
    residual = forcing - pushing - operate(velocity_ext, shear_resistance_map)
    spectrum, _ = transform_forward(residual, tables, None)
    components = residual.shape[0]
    for outer_step in range(OUTER):
        direction_ext = None
        energy_now = jnp.float32(1.0)
        for inner_step in range(INNER):
            if inner_step > 0:
                image_spectrum, curvature = transform_forward(image, tables, curvature_part)
                step_size = energy_now / curvature
                velocity_ext = velocity_ext + step_size * direction_ext
                spectrum = spectrum - step_size * image_spectrum
            filtered = spectrum * symbol[None]
            precond_ext, energy_next = transform_inverse(
                filtered, tables, jnp.sum(spectrum * filtered), prior_window_motion.shape
            )
            if inner_step == 0:
                direction_ext = precond_ext
            else:
                direction_ext = precond_ext + energy_next / energy_now * direction_ext
            energy_now = energy_next
            image = operate(direction_ext, shear_resistance_map)
            curvature_part = jnp.sum(direction_ext[inner_cells] * image)
        if outer_step < OUTER - 1:
            base_pressure = pressure_low + AUGMENT * divergence_region(velocity_ext)
            held = forcing - pressure_gradient(base_pressure) - operate(
                velocity_ext, shear_resistance_map
            )
            moving = (
                -pressure_gradient(AUGMENT * divergence_region(direction_ext)) - image
            )
            both, curvature = transform_forward(
                jnp.concatenate([held, moving], 0), tables, curvature_part
            )
            step_size = energy_now / curvature
            spectrum = both[:components] + step_size * both[components:]
        else:
            step_size = energy_now / global_sum(curvature_part)
        velocity_ext = velocity_ext + step_size * direction_ext
        spread_now = divergence_region(velocity_ext)
        pressure_low = pressure_low + AUGMENT * spread_now
    velocity = velocity_ext[:, 1 : owned_height_lines + 1, 1 : owned_depth_slices + 1, :]
    pressure = pressure_low[1:, 1:, :]
    return (velocity, pressure)


def solution(mesh):
    placed = (P(None, "row", "col", None), P("row", "col", None), P("row", "col", None))
    return jax.shard_map(
        per_device,
        mesh=mesh,
        in_specs=placed,
        out_specs=(P(None, "row", "col", None), P("row", "col", None)),
        check_vma=False,
    )
```

```python
import jax
import jax.numpy as jnp
from jax import lax
from jax.sharding import PartitionSpec as P

OUTER = 2
INNER = 2


PRECISE = lax.Precision.HIGHEST
ENABLE_SWITCH = 2.0
OFFSET_COUNT = 0.5
AUGMENT = 1.0
ANCHOR = 0.002
RAYLEIGH_NUMBER = 1.0
SMOOTHING = 2.0


def padded(cells, sides, width):
    for axis, dim in sides:
        count = lax.axis_size(axis)
        head = lax.slice_in_dim(cells, 0, width, axis=dim)
        tail = lax.slice_in_dim(cells, cells.shape[dim] - width, cells.shape[dim], axis=dim)
        cells = jnp.concatenate(
            [
                lax.ppermute(tail, axis, [(i, (i + 1) % count) for i in range(count)]),
                cells,
                lax.ppermute(head, axis, [((i + 1) % count, i) for i in range(count)]),
            ],
            axis=dim,
        )
    return cells


def surrounded(cells):
    rows = lax.axis_size("row")
    cols = lax.axis_size("col")

    def shifted(value, down, right):
        pairs = [
            (i * cols + j, ((i + down) % rows) * cols + (j + right) % cols)
            for i in range(rows)
            for j in range(cols)
        ]
        return lax.ppermute(value, ("row", "col"), pairs)

    low_y = from_behind(cells[:, -1:], "row", 1)
    high_y = from_behind(cells[:, :1], "row", -1)
    low_z = from_behind(cells[:, :, -1:], "col", 1)
    high_z = from_behind(cells[:, :, :1], "col", -1)
    low_low = shifted(cells[:, -1:, -1:], 1, 1)
    low_high = shifted(cells[:, -1:, :1], 1, -1)
    high_low = shifted(cells[:, :1, -1:], -1, 1)
    high_high = shifted(cells[:, :1, :1], -1, -1)
    top = jnp.concatenate([low_low, low_y, low_high], 2)
    middle = jnp.concatenate([low_z, cells, high_z], 2)
    bottom = jnp.concatenate([high_low, high_y, high_high], 2)
    return jnp.concatenate([top, middle, bottom], 1)


def global_sum(value):
    count = lax.axis_size("row") * lax.axis_size("col")
    spread = jnp.broadcast_to(value.reshape(1), (count,))
    gathered = lax.all_to_all(spread, ("row", "col"), 0, 0, tiled=True)
    return jnp.sum(gathered)


def from_behind(value, axis, steps):
    count = lax.axis_size(axis)
    pairs = [(source, (source + steps) % count) for source in range(count)]
    return lax.ppermute(value, axis, pairs)


def cas_matrix(extent):
    index = jnp.arange(extent, dtype=jnp.int32)
    phase = index[:, None] * index[None, :] % extent
    angle = 2.0 * jnp.pi / extent * phase.astype(jnp.float32)
    return jnp.cos(angle) + jnp.sin(angle)


def widened(table, pieces):
    extent = table.shape[0]
    width = extent // pieces
    index = jnp.arange(pieces * (width + 2), dtype=jnp.int32)
    rows = (index // (width + 2)) * width + index % (width + 2) - 1
    return table[rows % extent]


def eigen_row(number, offset_index, extent):
    index = offset_index + jnp.arange(number, dtype=jnp.int32)
    return 2.0 - 2.0 * jnp.cos(2.0 * jnp.pi / extent * index.astype(jnp.float32))


def exchange(cells, partial, axis, split_axis, concat_axis):
    if partial is None:
        moved = lax.all_to_all(cells, axis, split_axis, concat_axis, tiled=True)
        return moved, None
    count = lax.axis_size(axis)
    rider = jnp.broadcast_to(partial.astype(cells.dtype), (1,) + cells.shape[1:])
    moved = lax.all_to_all(
        jnp.concatenate([cells, rider], 0), axis, split_axis, concat_axis, tiled=True
    )
    rider = moved[-1]
    pieces = rider.shape[concat_axis - 1] // count
    picks = tuple(
        slice(0, None, pieces) if dim == concat_axis - 1 else slice(0, 1)
        for dim in range(rider.ndim)
    )
    return moved[:-1], jnp.sum(rider[picks])


def spectral_symbol(shape):
    row_count = lax.axis_size("row")
    col_count = lax.axis_size("col")
    components, owned_height_lines, owned_depth_slices, period_extent_first = shape
    ylength = owned_height_lines * row_count
    zlength = owned_depth_slices * col_count
    normal_factor = 1.0 / (period_extent_first * ylength * zlength)
    xpiece = period_extent_first // row_count
    ypiece = ylength // col_count
    zeigen = eigen_row(zlength, 0, zlength)
    yeigen = eigen_row(ypiece, lax.axis_index("col") * ypiece, ylength)
    xeigen = eigen_row(xpiece, lax.axis_index("row") * xpiece, period_extent_first)
    mixed_eigen = (yeigen[:, None] + xeigen[None, :]).reshape(-1)
    return normal_factor / (SMOOTHING * (zeigen[:, None] + mixed_eigen[None, :]) + ANCHOR)


def transform_forward(residual, tables, partial):
    xtable, ytable, ztable = tables
    row_count = lax.axis_size("row")
    components, owned_height_lines, owned_depth_slices, period_extent_first = residual.shape
    ylength = owned_height_lines * row_count
    xpiece = period_extent_first // row_count
    spectrum = jnp.einsum("kx,cyzx->cykz", xtable, residual, precision=PRECISE).reshape(
        components, owned_height_lines, period_extent_first * owned_depth_slices
    )
    spectrum, partial = exchange(spectrum, partial, "row", 2, 1)
    spectrum = jnp.einsum(
        "ky,cyxz->czkx",
        ytable,
        spectrum.reshape(components, ylength, xpiece, owned_depth_slices),
        precision=PRECISE,
    ).reshape(components, owned_depth_slices, ylength * xpiece)
    spectrum, partial = exchange(spectrum, partial, "col", 2, 1)
    return jnp.einsum("kz,czm->ckm", ztable, spectrum, precision=PRECISE), partial


def transform_inverse(filtered, tables, partial, shape):
    xtable, ytable, ztable = tables
    row_count = lax.axis_size("row")
    col_count = lax.axis_size("col")
    components, owned_height_lines, owned_depth_slices, period_extent_first = shape
    ylength = owned_height_lines * row_count
    xpiece = period_extent_first // row_count
    zwide = widened(ztable, col_count)
    ywide = widened(ytable, row_count)
    spectrum = jnp.einsum("kz,czm->ckm", zwide, filtered, precision=PRECISE)
    spectrum, partial = exchange(spectrum, partial, "col", 1, 2)
    spectrum = jnp.einsum(
        "ky,czyx->ckxz",
        ywide,
        spectrum.reshape(components, owned_depth_slices + 2, ylength, xpiece),
        precision=PRECISE,
    ).reshape(components, row_count * (owned_height_lines + 2), xpiece * (owned_depth_slices + 2))
    spectrum, partial = exchange(spectrum, partial, "row", 1, 2)
    return jnp.einsum(
        "kx,cyxz->cyzk",
        xtable,
        spectrum.reshape(
            components, owned_height_lines + 2, period_extent_first, owned_depth_slices + 2
        ),
        precision=PRECISE,
    ), partial


def forward(extended, direction):
    owned_height_lines = extended.shape[-3] - 2
    owned_depth_slices = extended.shape[-2] - 2
    root = extended[..., : owned_height_lines + 1, : owned_depth_slices + 1, :]
    if direction == 0:
        return jnp.roll(root, -1, -1) - root
    if direction == 1:
        return extended[..., 1 : owned_height_lines + 2, : owned_depth_slices + 1, :] - root
    return extended[..., : owned_height_lines + 1, 1 : owned_depth_slices + 2, :] - root


def backward(region, direction):
    center = region[..., 1:, 1:, :]
    if direction == 0:
        return center - jnp.roll(center, 1, -1)
    if direction == 1:
        return center - region[..., :-1, 1:, :]
    return center - region[..., 1:, :-1, :]


def extend(field):
    return padded(field, (("row", 1), ("col", 2)), 1)


def lower_region(pressure):
    below_y = from_behind(pressure[-1:], "row", 1)
    below_z = from_behind(pressure[:, -1:], "col", 1)
    corner = jnp.zeros((1, 1, pressure.shape[2]), jnp.float32)
    upper_band = jnp.concatenate([corner, below_y], 1)
    main_band = jnp.concatenate([below_z, pressure], 1)
    return jnp.concatenate([upper_band, main_band], 0)


def operate(extended, shear_resistance_map):
    owned_height_lines = extended.shape[1] - 2
    owned_depth_slices = extended.shape[2] - 2
    gradients = [[forward(extended[target], source) for source in range(3)] for target in range(3)]
    spread = gradients[0][0] + gradients[1][1] + gradients[2][2]
    result = []
    for target in range(3):
        summed = (
            ANCHOR * extended[target, 1 : owned_height_lines + 1, 1 : owned_depth_slices + 1, :]
        )
        for source in range(3):
            fluxes = shear_resistance_map * (gradients[target][source] + gradients[source][target])
            if target == source:
                fluxes = fluxes + AUGMENT * spread
            summed = summed - backward(fluxes, source)
        result.append(summed)
    return jnp.stack(result)


def pressure_gradient(region):
    return jnp.stack([-backward(region, target) for target in range(3)])


def divergence_region(extended):
    return forward(extended[0], 0) + forward(extended[1], 1) + forward(extended[2], 2)


def per_device(prior_window_motion, prior_window_stress, heat_scalar):
    owned_height_lines, owned_depth_slices, period_extent_first = heat_scalar.shape
    tables = (
        cas_matrix(period_extent_first),
        cas_matrix(owned_height_lines * lax.axis_size("row")),
        cas_matrix(owned_depth_slices * lax.axis_size("col")),
    )
    stacked_fields = jnp.concatenate(
        [prior_window_motion, prior_window_stress[None], heat_scalar[None]], 0
    )
    extended = surrounded(stacked_fields)
    shear_resistance_map = jnp.exp(
        ENABLE_SWITCH
        * (
            1.0
            / (extended[4, : owned_height_lines + 1, : owned_depth_slices + 1, :] + OFFSET_COUNT)
            - 1.0 / (0.5 + OFFSET_COUNT)
        )
    )
    thermal_lift = RAYLEIGH_NUMBER * (heat_scalar - 0.5)
    zeroes = jnp.zeros_like(thermal_lift)
    forcing = jnp.stack([zeroes, zeroes, thermal_lift])
    velocity_ext = extended[0:3]
    pressure_low = extended[3, : owned_height_lines + 1, : owned_depth_slices + 1, :]
    symbol = spectral_symbol(prior_window_motion.shape)
    inner_cells = (slice(None), slice(1, owned_height_lines + 1), slice(1, owned_depth_slices + 1))
    for outer_step in range(OUTER):
        pushing = pressure_gradient(pressure_low)
        residual = forcing - pushing - operate(velocity_ext, shear_resistance_map)
        spectrum, _ = transform_forward(residual, tables, None)
        direction_ext = None
        energy_now = jnp.float32(1.0)
        for inner_step in range(INNER):
            if inner_step > 0:
                image_spectrum, curvature = transform_forward(image, tables, curvature_part)
                step_size = energy_now / curvature
                velocity_ext = velocity_ext + step_size * direction_ext
                spectrum = spectrum - step_size * image_spectrum
            filtered = spectrum * symbol[None]
            precond_ext, energy_next = transform_inverse(
                filtered, tables, jnp.sum(spectrum * filtered), prior_window_motion.shape
            )
            if inner_step == 0:
                direction_ext = precond_ext
            else:
                direction_ext = precond_ext + energy_next / energy_now * direction_ext
            energy_now = energy_next
            image = operate(direction_ext, shear_resistance_map)
            curvature_part = jnp.sum(direction_ext[inner_cells] * image)
        step_size = energy_now / global_sum(curvature_part)
        velocity_ext = velocity_ext + step_size * direction_ext
        spread_now = divergence_region(velocity_ext)
        pressure_low = pressure_low + AUGMENT * spread_now
    velocity = velocity_ext[:, 1 : owned_height_lines + 1, 1 : owned_depth_slices + 1, :]
    pressure = pressure_low[1:, 1:, :]
    return (velocity, pressure)


def solution(mesh):
    placed = (P(None, "row", "col", None), P("row", "col", None), P("row", "col", None))
    return jax.shard_map(
        per_device,
        mesh=mesh,
        in_specs=placed,
        out_specs=(P(None, "row", "col", None), P("row", "col", None)),
        check_vma=False,
    )
```

```python
import jax
import jax.numpy as jnp
from jax import lax
from jax.sharding import PartitionSpec as P

OUTER = 2
INNER = 2


PRECISE = lax.Precision.HIGHEST
ENABLE_SWITCH = 2.0
OFFSET_COUNT = 0.5
AUGMENT = 1.0
ANCHOR = 0.002
RAYLEIGH_NUMBER = 1.0
SMOOTHING = 2.0


def padded(cells, sides, width):
    for axis, dim in sides:
        count = lax.axis_size(axis)
        head = lax.slice_in_dim(cells, 0, width, axis=dim)
        tail = lax.slice_in_dim(cells, cells.shape[dim] - width, cells.shape[dim], axis=dim)
        cells = jnp.concatenate(
            [
                lax.ppermute(tail, axis, [(i, (i + 1) % count) for i in range(count)]),
                cells,
                lax.ppermute(head, axis, [((i + 1) % count, i) for i in range(count)]),
            ],
            axis=dim,
        )
    return cells


def global_sum(value):
    count = lax.axis_size("row") * lax.axis_size("col")
    spread = jnp.broadcast_to(value.reshape(1), (count,))
    gathered = lax.all_to_all(spread, ("row", "col"), 0, 0, tiled=True)
    return jnp.sum(gathered)


def from_behind(value, axis, steps):
    count = lax.axis_size(axis)
    pairs = [(source, (source + steps) % count) for source in range(count)]
    return lax.ppermute(value, axis, pairs)


def cas_matrix(extent):
    index = jnp.arange(extent, dtype=jnp.int32)
    phase = index[:, None] * index[None, :] % extent
    angle = 2.0 * jnp.pi / extent * phase.astype(jnp.float32)
    return jnp.cos(angle) + jnp.sin(angle)


def widened(table, pieces):
    extent = table.shape[0]
    width = extent // pieces
    index = jnp.arange(pieces * (width + 2), dtype=jnp.int32)
    rows = (index // (width + 2)) * width + index % (width + 2) - 1
    return table[rows % extent]


def eigen_row(number, offset_index, extent):
    index = offset_index + jnp.arange(number, dtype=jnp.int32)
    return 2.0 - 2.0 * jnp.cos(2.0 * jnp.pi / extent * index.astype(jnp.float32))


def exchange(cells, partial, axis, split_axis, concat_axis):
    if partial is None:
        moved = lax.all_to_all(cells, axis, split_axis, concat_axis, tiled=True)
        return moved, None
    count = lax.axis_size(axis)
    rider = jnp.broadcast_to(partial.astype(cells.dtype), (1,) + cells.shape[1:])
    moved = lax.all_to_all(
        jnp.concatenate([cells, rider], 0), axis, split_axis, concat_axis, tiled=True
    )
    arrived = jnp.moveaxis(moved[-1], concat_axis - 1, 0)
    arrived = arrived.reshape(count, arrived.shape[0] // count, -1)[:, 0, 0]
    return moved[:-1], jnp.sum(arrived)


def carried(cells, axis, split_axis, concat_axis):
    count = lax.axis_size(axis)
    moved = lax.all_to_all(cells, axis, split_axis, concat_axis, tiled=True)
    arrived = jnp.moveaxis(moved[-1], concat_axis - 1, 0)
    arrived = arrived.reshape(count, arrived.shape[0] // count, -1)[:, 0, 0]
    return moved[:-1], jnp.sum(arrived)


def with_pulse(cells, partial, dim):
    place = lax.broadcasted_iota(jnp.int32, (1,) + cells.shape[1:], dim)
    pulse = jnp.where(place == 0, partial.astype(cells.dtype), jnp.zeros((), cells.dtype))
    return jnp.concatenate([cells, pulse], 0)


def spectral_symbol(shape):
    row_count = lax.axis_size("row")
    col_count = lax.axis_size("col")
    components, owned_height_lines, owned_depth_slices, period_extent_first = shape
    ylength = owned_height_lines * row_count
    zlength = owned_depth_slices * col_count
    normal_factor = 1.0 / (period_extent_first * ylength * zlength)
    xpiece = period_extent_first // row_count
    ypiece = ylength // col_count
    zeigen = eigen_row(zlength, 0, zlength)
    yeigen = eigen_row(ypiece, lax.axis_index("col") * ypiece, ylength)
    xeigen = eigen_row(xpiece, lax.axis_index("row") * xpiece, period_extent_first)
    mixed_eigen = (yeigen[:, None] + xeigen[None, :]).reshape(-1)
    return normal_factor / (SMOOTHING * (zeigen[:, None] + mixed_eigen[None, :]) + ANCHOR)


def transform_forward(residual, tables, partial):
    xtable, ytable, ztable = tables
    row_count = lax.axis_size("row")
    components, owned_height_lines, owned_depth_slices, period_extent_first = residual.shape
    ylength = owned_height_lines * row_count
    xpiece = period_extent_first // row_count
    if partial is not None:
        residual = with_pulse(residual, partial, 3)
    spectrum = jnp.einsum("kx,cyzx->cykz", xtable, residual, precision=PRECISE).reshape(
        residual.shape[0], owned_height_lines, period_extent_first * owned_depth_slices
    )
    if partial is None:
        spectrum, partial = exchange(spectrum, None, "row", 2, 1)
    else:
        spectrum, partial = carried(spectrum, "row", 2, 1)
    spectrum = jnp.einsum(
        "ky,cyxz->czkx",
        ytable,
        spectrum.reshape(components, ylength, xpiece, owned_depth_slices),
        precision=PRECISE,
    ).reshape(components, owned_depth_slices, ylength * xpiece)
    spectrum, partial = exchange(spectrum, partial, "col", 2, 1)
    return jnp.einsum("kz,czm->ckm", ztable, spectrum, precision=PRECISE), partial


def transform_inverse(filtered, tables, partial, shape):
    xtable, ytable, ztable = tables
    row_count = lax.axis_size("row")
    col_count = lax.axis_size("col")
    components, owned_height_lines, owned_depth_slices, period_extent_first = shape
    ylength = owned_height_lines * row_count
    xpiece = period_extent_first // row_count
    zwide = widened(ztable, col_count)
    ywide = widened(ytable, row_count)
    spectrum = jnp.einsum(
        "kz,czm->ckm", zwide, with_pulse(filtered, partial, 1), precision=PRECISE
    )
    spectrum, partial = carried(spectrum, "col", 1, 2)
    spectrum = jnp.einsum(
        "ky,czyx->ckxz",
        ywide,
        spectrum.reshape(components, owned_depth_slices + 2, ylength, xpiece),
        precision=PRECISE,
    ).reshape(components, row_count * (owned_height_lines + 2), xpiece * (owned_depth_slices + 2))
    spectrum, partial = exchange(spectrum, partial, "row", 1, 2)
    return jnp.einsum(
        "kx,cyxz->cyzk",
        xtable,
        spectrum.reshape(
            components, owned_height_lines + 2, period_extent_first, owned_depth_slices + 2
        ),
        precision=PRECISE,
    ), partial


def forward(extended, direction):
    owned_height_lines = extended.shape[-3] - 2
    owned_depth_slices = extended.shape[-2] - 2
    root = extended[..., : owned_height_lines + 1, : owned_depth_slices + 1, :]
    if direction == 0:
        return jnp.roll(root, -1, -1) - root
    if direction == 1:
        return extended[..., 1 : owned_height_lines + 2, : owned_depth_slices + 1, :] - root
    return extended[..., : owned_height_lines + 1, 1 : owned_depth_slices + 2, :] - root


def backward(region, direction):
    center = region[..., 1:, 1:, :]
    if direction == 0:
        return center - jnp.roll(center, 1, -1)
    if direction == 1:
        return center - region[..., :-1, 1:, :]
    return center - region[..., 1:, :-1, :]


def extend(field):
    return padded(field, (("row", 1), ("col", 2)), 1)


def lower_region(pressure):
    below_y = from_behind(pressure[-1:], "row", 1)
    below_z = from_behind(pressure[:, -1:], "col", 1)
    corner = jnp.zeros((1, 1, pressure.shape[2]), jnp.float32)
    upper_band = jnp.concatenate([corner, below_y], 1)
    main_band = jnp.concatenate([below_z, pressure], 1)
    return jnp.concatenate([upper_band, main_band], 0)


def operate(extended, shear_resistance_map):
    owned_height_lines = extended.shape[1] - 2
    owned_depth_slices = extended.shape[2] - 2
    gradients = [[forward(extended[target], source) for source in range(3)] for target in range(3)]
    spread = gradients[0][0] + gradients[1][1] + gradients[2][2]
    result = []
    for target in range(3):
        summed = (
            ANCHOR * extended[target, 1 : owned_height_lines + 1, 1 : owned_depth_slices + 1, :]
        )
        for source in range(3):
            fluxes = shear_resistance_map * (gradients[target][source] + gradients[source][target])
            if target == source:
                fluxes = fluxes + AUGMENT * spread
            summed = summed - backward(fluxes, source)
        result.append(summed)
    return jnp.stack(result)


def pressure_gradient(region):
    return jnp.stack([-backward(region, target) for target in range(3)])


def divergence_region(extended):
    return forward(extended[0], 0) + forward(extended[1], 1) + forward(extended[2], 2)


def per_device(prior_window_motion, prior_window_stress, heat_scalar):
    owned_height_lines, owned_depth_slices, period_extent_first = heat_scalar.shape
    tables = (
        cas_matrix(period_extent_first),
        cas_matrix(owned_height_lines * lax.axis_size("row")),
        cas_matrix(owned_depth_slices * lax.axis_size("col")),
    )
    stacked_fields = jnp.concatenate(
        [prior_window_motion, prior_window_stress[None], heat_scalar[None]], 0
    )
    extended = padded(stacked_fields, (("row", 1), ("col", 2)), 1)
    shear_resistance_map = jnp.exp(
        ENABLE_SWITCH
        * (
            1.0
            / (extended[4, : owned_height_lines + 1, : owned_depth_slices + 1, :] + OFFSET_COUNT)
            - 1.0 / (0.5 + OFFSET_COUNT)
        )
    )
    thermal_lift = RAYLEIGH_NUMBER * (heat_scalar - 0.5)
    zeroes = jnp.zeros_like(thermal_lift)
    forcing = jnp.stack([zeroes, zeroes, thermal_lift])
    velocity_ext = extended[0:3]
    pressure_low = extended[3, : owned_height_lines + 1, : owned_depth_slices + 1, :]
    symbol = spectral_symbol(prior_window_motion.shape)
    inner_cells = (slice(None), slice(1, owned_height_lines + 1), slice(1, owned_depth_slices + 1))
    for outer_step in range(OUTER):
        pushing = pressure_gradient(pressure_low)
        residual = forcing - pushing - operate(velocity_ext, shear_resistance_map)
        spectrum, _ = transform_forward(residual, tables, None)
        direction_ext = None
        energy_now = jnp.float32(1.0)
        for inner_step in range(INNER):
            if inner_step > 0:
                image_spectrum, curvature = transform_forward(image, tables, curvature_part)
                step_size = energy_now / curvature
                velocity_ext = velocity_ext + step_size * direction_ext
                spectrum = spectrum - step_size * image_spectrum
            filtered = spectrum * symbol[None]
            precond_ext, energy_next = transform_inverse(
                filtered, tables, jnp.sum(spectrum * filtered), prior_window_motion.shape
            )
            if inner_step == 0:
                direction_ext = precond_ext
            else:
                direction_ext = precond_ext + energy_next / energy_now * direction_ext
            energy_now = energy_next
            image = operate(direction_ext, shear_resistance_map)
            curvature_part = jnp.sum(direction_ext[inner_cells] * image)
        step_size = energy_now / global_sum(curvature_part)
        velocity_ext = velocity_ext + step_size * direction_ext
        spread_now = divergence_region(velocity_ext)
        pressure_low = pressure_low + AUGMENT * spread_now
    velocity = velocity_ext[:, 1 : owned_height_lines + 1, 1 : owned_depth_slices + 1, :]
    pressure = pressure_low[1:, 1:, :]
    return (velocity, pressure)


def solution(mesh):
    placed = (P(None, "row", "col", None), P("row", "col", None), P("row", "col", None))
    return jax.shard_map(
        per_device,
        mesh=mesh,
        in_specs=placed,
        out_specs=(P(None, "row", "col", None), P("row", "col", None)),
        check_vma=False,
    )
```

```python
import jax
import jax.numpy as jnp
from jax import lax
from jax.sharding import PartitionSpec as P

OUTER = 2
INNER = 2


PRECISE = lax.Precision.HIGHEST
ENABLE_SWITCH = 2.0
OFFSET_COUNT = 0.5
AUGMENT = 1.0
ANCHOR = 0.002
RAYLEIGH_NUMBER = 1.0
SMOOTHING = 2.0


def padded(cells, sides, width):
    for axis, dim in sides:
        count = lax.axis_size(axis)
        head = lax.slice_in_dim(cells, 0, width, axis=dim)
        tail = lax.slice_in_dim(cells, cells.shape[dim] - width, cells.shape[dim], axis=dim)
        cells = jnp.concatenate(
            [
                lax.ppermute(tail, axis, [(i, (i + 1) % count) for i in range(count)]),
                cells,
                lax.ppermute(head, axis, [((i + 1) % count, i) for i in range(count)]),
            ],
            axis=dim,
        )
    return cells


def global_sum(value):
    count = lax.axis_size("row") * lax.axis_size("col")
    spread = jnp.broadcast_to(value.reshape(1), (count,))
    gathered = lax.all_to_all(spread, ("row", "col"), 0, 0, tiled=True)
    return jnp.sum(gathered)


def from_behind(value, axis, steps):
    count = lax.axis_size(axis)
    pairs = [(source, (source + steps) % count) for source in range(count)]
    return lax.ppermute(value, axis, pairs)


def cas_matrix(extent):
    index = jnp.arange(extent, dtype=jnp.int32)
    phase = index[:, None] * index[None, :] % extent
    angle = 2.0 * jnp.pi / extent * phase.astype(jnp.float32)
    return jnp.cos(angle) + jnp.sin(angle)


def widened(table, pieces):
    extent = table.shape[0]
    width = extent // pieces
    index = jnp.arange(pieces * (width + 2), dtype=jnp.int32)
    rows = (index // (width + 2)) * width + index % (width + 2) - 1
    return table[rows % extent]


def eigen_row(number, offset_index, extent):
    index = offset_index + jnp.arange(number, dtype=jnp.int32)
    return 2.0 - 2.0 * jnp.cos(2.0 * jnp.pi / extent * index.astype(jnp.float32))


def exchange(cells, partial, axis, split_axis, concat_axis):
    if partial is None:
        moved = lax.all_to_all(cells, axis, split_axis, concat_axis, tiled=True)
        return moved, None
    count = lax.axis_size(axis)
    rider = jnp.broadcast_to(partial.astype(cells.dtype), (1,) + cells.shape[1:])
    moved = lax.all_to_all(
        jnp.concatenate([cells, rider], 0), axis, split_axis, concat_axis, tiled=True
    )
    arrived = jnp.moveaxis(moved[-1], concat_axis - 1, 0)
    arrived = arrived.reshape(count, arrived.shape[0] // count, -1)[:, 0, 0]
    return moved[:-1], jnp.sum(arrived)


def carried(cells, axis, split_axis, concat_axis):
    count = lax.axis_size(axis)
    moved = lax.all_to_all(cells, axis, split_axis, concat_axis, tiled=True)
    arrived = jnp.moveaxis(moved[-1], concat_axis - 1, 0)
    arrived = arrived.reshape(count, arrived.shape[0] // count, -1)[:, 0, 0]
    return moved[:-1], jnp.sum(arrived)


def with_pulse(cells, partial, dim):
    place = lax.broadcasted_iota(jnp.int32, (1,) + cells.shape[1:], dim)
    pulse = jnp.where(place == 0, partial.astype(cells.dtype), jnp.zeros((), cells.dtype))
    return jnp.concatenate([cells, pulse], 0)


def spectral_symbol(shape):
    row_count = lax.axis_size("row")
    col_count = lax.axis_size("col")
    components, owned_height_lines, owned_depth_slices, period_extent_first = shape
    ylength = owned_height_lines * row_count
    zlength = owned_depth_slices * col_count
    normal_factor = 1.0 / (period_extent_first * ylength * zlength)
    xpiece = period_extent_first // row_count
    ypiece = ylength // col_count
    zeigen = eigen_row(zlength, 0, zlength)
    yeigen = eigen_row(ypiece, lax.axis_index("col") * ypiece, ylength)
    xeigen = eigen_row(xpiece, lax.axis_index("row") * xpiece, period_extent_first)
    mixed_eigen = (yeigen[:, None] + xeigen[None, :]).reshape(-1)
    return normal_factor / (SMOOTHING * (zeigen[:, None] + mixed_eigen[None, :]) + ANCHOR)


def transform_forward(residual, tables, partial):
    xtable, ytable, ztable = tables
    row_count = lax.axis_size("row")
    components, owned_height_lines, owned_depth_slices, period_extent_first = residual.shape
    ylength = owned_height_lines * row_count
    xpiece = period_extent_first // row_count
    if partial is not None:
        residual = with_pulse(residual, partial, 3)
    spectrum = jnp.einsum("kx,cyzx->cykz", xtable, residual, precision=PRECISE).reshape(
        residual.shape[0], owned_height_lines, period_extent_first * owned_depth_slices
    )
    if partial is None:
        spectrum, _ = exchange(spectrum, None, "row", 2, 1)
        lines = spectrum.reshape(components, ylength, xpiece, owned_depth_slices)
    else:
        spectrum, partial = carried(spectrum, "row", 2, 1)
        lines = with_pulse(
            spectrum.reshape(components, ylength, xpiece, owned_depth_slices), partial, 1
        )
    spectrum = jnp.einsum("ky,cyxz->czkx", ytable, lines, precision=PRECISE).reshape(
        lines.shape[0], owned_depth_slices, ylength * xpiece
    )
    if partial is None:
        spectrum, _ = exchange(spectrum, None, "col", 2, 1)
    else:
        spectrum, partial = carried(spectrum, "col", 2, 1)
    return jnp.einsum("kz,czm->ckm", ztable, spectrum, precision=PRECISE), partial


def transform_inverse(filtered, tables, partial, shape):
    xtable, ytable, ztable = tables
    row_count = lax.axis_size("row")
    col_count = lax.axis_size("col")
    components, owned_height_lines, owned_depth_slices, period_extent_first = shape
    ylength = owned_height_lines * row_count
    xpiece = period_extent_first // row_count
    zwide = widened(ztable, col_count)
    ywide = widened(ytable, row_count)
    spectrum = jnp.einsum(
        "kz,czm->ckm", zwide, with_pulse(filtered, partial, 1), precision=PRECISE
    )
    spectrum, partial = carried(spectrum, "col", 1, 2)
    lines = with_pulse(
        spectrum.reshape(components, owned_depth_slices + 2, ylength, xpiece), partial, 2
    )
    spectrum = jnp.einsum("ky,czyx->ckxz", ywide, lines, precision=PRECISE).reshape(
        components + 1, row_count * (owned_height_lines + 2), xpiece * (owned_depth_slices + 2)
    )
    spectrum, partial = carried(spectrum, "row", 1, 2)
    return jnp.einsum(
        "kx,cyxz->cyzk",
        xtable,
        spectrum.reshape(
            components, owned_height_lines + 2, period_extent_first, owned_depth_slices + 2
        ),
        precision=PRECISE,
    ), partial


def forward(extended, direction):
    owned_height_lines = extended.shape[-3] - 2
    owned_depth_slices = extended.shape[-2] - 2
    root = extended[..., : owned_height_lines + 1, : owned_depth_slices + 1, :]
    if direction == 0:
        return jnp.roll(root, -1, -1) - root
    if direction == 1:
        return extended[..., 1 : owned_height_lines + 2, : owned_depth_slices + 1, :] - root
    return extended[..., : owned_height_lines + 1, 1 : owned_depth_slices + 2, :] - root


def backward(region, direction):
    center = region[..., 1:, 1:, :]
    if direction == 0:
        return center - jnp.roll(center, 1, -1)
    if direction == 1:
        return center - region[..., :-1, 1:, :]
    return center - region[..., 1:, :-1, :]


def extend(field):
    return padded(field, (("row", 1), ("col", 2)), 1)


def lower_region(pressure):
    below_y = from_behind(pressure[-1:], "row", 1)
    below_z = from_behind(pressure[:, -1:], "col", 1)
    corner = jnp.zeros((1, 1, pressure.shape[2]), jnp.float32)
    upper_band = jnp.concatenate([corner, below_y], 1)
    main_band = jnp.concatenate([below_z, pressure], 1)
    return jnp.concatenate([upper_band, main_band], 0)


def operate(extended, shear_resistance_map):
    owned_height_lines = extended.shape[1] - 2
    owned_depth_slices = extended.shape[2] - 2
    gradients = [[forward(extended[target], source) for source in range(3)] for target in range(3)]
    spread = gradients[0][0] + gradients[1][1] + gradients[2][2]
    result = []
    for target in range(3):
        summed = (
            ANCHOR * extended[target, 1 : owned_height_lines + 1, 1 : owned_depth_slices + 1, :]
        )
        for source in range(3):
            fluxes = shear_resistance_map * (gradients[target][source] + gradients[source][target])
            if target == source:
                fluxes = fluxes + AUGMENT * spread
            summed = summed - backward(fluxes, source)
        result.append(summed)
    return jnp.stack(result)


def pressure_gradient(region):
    return jnp.stack([-backward(region, target) for target in range(3)])


def divergence_region(extended):
    return forward(extended[0], 0) + forward(extended[1], 1) + forward(extended[2], 2)


def per_device(prior_window_motion, prior_window_stress, heat_scalar):
    owned_height_lines, owned_depth_slices, period_extent_first = heat_scalar.shape
    tables = (
        cas_matrix(period_extent_first),
        cas_matrix(owned_height_lines * lax.axis_size("row")),
        cas_matrix(owned_depth_slices * lax.axis_size("col")),
    )
    stacked_fields = jnp.concatenate(
        [prior_window_motion, prior_window_stress[None], heat_scalar[None]], 0
    )
    extended = padded(stacked_fields, (("row", 1), ("col", 2)), 1)
    shear_resistance_map = jnp.exp(
        ENABLE_SWITCH
        * (
            1.0
            / (extended[4, : owned_height_lines + 1, : owned_depth_slices + 1, :] + OFFSET_COUNT)
            - 1.0 / (0.5 + OFFSET_COUNT)
        )
    )
    thermal_lift = RAYLEIGH_NUMBER * (heat_scalar - 0.5)
    zeroes = jnp.zeros_like(thermal_lift)
    forcing = jnp.stack([zeroes, zeroes, thermal_lift])
    velocity_ext = extended[0:3]
    pressure_low = extended[3, : owned_height_lines + 1, : owned_depth_slices + 1, :]
    symbol = spectral_symbol(prior_window_motion.shape)
    inner_cells = (slice(None), slice(1, owned_height_lines + 1), slice(1, owned_depth_slices + 1))
    for outer_step in range(OUTER):
        pushing = pressure_gradient(pressure_low)
        residual = forcing - pushing - operate(velocity_ext, shear_resistance_map)
        spectrum, _ = transform_forward(residual, tables, None)
        direction_ext = None
        energy_now = jnp.float32(1.0)
        for inner_step in range(INNER):
            if inner_step > 0:
                image_spectrum, curvature = transform_forward(image, tables, curvature_part)
                step_size = energy_now / curvature
                velocity_ext = velocity_ext + step_size * direction_ext
                spectrum = spectrum - step_size * image_spectrum
            filtered = spectrum * symbol[None]
            precond_ext, energy_next = transform_inverse(
                filtered, tables, jnp.sum(spectrum * filtered), prior_window_motion.shape
            )
            if inner_step == 0:
                direction_ext = precond_ext
            else:
                direction_ext = precond_ext + energy_next / energy_now * direction_ext
            energy_now = energy_next
            image = operate(direction_ext, shear_resistance_map)
            curvature_part = jnp.sum(direction_ext[inner_cells] * image)
        step_size = energy_now / global_sum(curvature_part)
        velocity_ext = velocity_ext + step_size * direction_ext
        spread_now = divergence_region(velocity_ext)
        pressure_low = pressure_low + AUGMENT * spread_now
    velocity = velocity_ext[:, 1 : owned_height_lines + 1, 1 : owned_depth_slices + 1, :]
    pressure = pressure_low[1:, 1:, :]
    return (velocity, pressure)


def solution(mesh):
    placed = (P(None, "row", "col", None), P("row", "col", None), P("row", "col", None))
    return jax.shard_map(
        per_device,
        mesh=mesh,
        in_specs=placed,
        out_specs=(P(None, "row", "col", None), P("row", "col", None)),
        check_vma=False,
    )
```

```python
import jax
import jax.numpy as jnp
from jax import lax
from jax.sharding import PartitionSpec as P

OUTER = 2
INNER = 2


PRECISE = lax.Precision.HIGHEST
ENABLE_SWITCH = 2.0
OFFSET_COUNT = 0.5
AUGMENT = 1.0
ANCHOR = 0.002
RAYLEIGH_NUMBER = 1.0
SMOOTHING = 2.0


def padded(cells, sides, width):
    for axis, dim in sides:
        count = lax.axis_size(axis)
        head = lax.slice_in_dim(cells, 0, width, axis=dim)
        tail = lax.slice_in_dim(cells, cells.shape[dim] - width, cells.shape[dim], axis=dim)
        cells = jnp.concatenate(
            [
                lax.ppermute(tail, axis, [(i, (i + 1) % count) for i in range(count)]),
                cells,
                lax.ppermute(head, axis, [((i + 1) % count, i) for i in range(count)]),
            ],
            axis=dim,
        )
    return cells


def global_sum(value):
    count = lax.axis_size("row") * lax.axis_size("col")
    spread = jnp.broadcast_to(value.reshape(1), (count,))
    gathered = lax.all_to_all(spread, ("row", "col"), 0, 0, tiled=True)
    return jnp.sum(gathered)


def from_behind(value, axis, steps):
    count = lax.axis_size(axis)
    pairs = [(source, (source + steps) % count) for source in range(count)]
    return lax.ppermute(value, axis, pairs)


def cas_matrix(extent):
    index = jnp.arange(extent, dtype=jnp.int32)
    phase = index[:, None] * index[None, :] % extent
    angle = 2.0 * jnp.pi / extent * phase.astype(jnp.float32)
    return jnp.cos(angle) + jnp.sin(angle)


def widened(table, pieces):
    extent = table.shape[0]
    width = extent // pieces
    index = jnp.arange(pieces * (width + 2), dtype=jnp.int32)
    rows = (index // (width + 2)) * width + index % (width + 2) - 1
    return table[rows % extent]


def eigen_row(number, offset_index, extent):
    index = offset_index + jnp.arange(number, dtype=jnp.int32)
    return 2.0 - 2.0 * jnp.cos(2.0 * jnp.pi / extent * index.astype(jnp.float32))


def exchange(cells, partial, axis, split_axis, concat_axis):
    if partial is None:
        moved = lax.all_to_all(cells, axis, split_axis, concat_axis, tiled=True)
        return moved, None
    count = lax.axis_size(axis)
    rider = jnp.broadcast_to(partial.astype(cells.dtype), (1,) + cells.shape[1:])
    moved = lax.all_to_all(
        jnp.concatenate([cells, rider], 0), axis, split_axis, concat_axis, tiled=True
    )
    arrived = jnp.moveaxis(moved[-1], concat_axis - 1, 0)
    arrived = arrived.reshape(count, arrived.shape[0] // count, -1)[:, 0, 0]
    return moved[:-1], jnp.sum(arrived)


def carried(cells, axis, split_axis, concat_axis):
    count = lax.axis_size(axis)
    moved = lax.all_to_all(cells, axis, split_axis, concat_axis, tiled=True)
    rider = moved[-1]
    pieces = rider.shape[concat_axis - 1] // count
    picks = tuple(
        slice(0, None, pieces) if dim == concat_axis - 1 else slice(0, 1)
        for dim in range(rider.ndim)
    )
    return moved[:-1], jnp.sum(rider[picks])


def with_pulse(cells, partial, dim):
    place = lax.broadcasted_iota(jnp.int32, (1,) + cells.shape[1:], dim)
    pulse = jnp.where(place == 0, partial.astype(cells.dtype), jnp.zeros((), cells.dtype))
    return jnp.concatenate([cells, pulse], 0)


def spectral_symbol(shape):
    row_count = lax.axis_size("row")
    col_count = lax.axis_size("col")
    components, owned_height_lines, owned_depth_slices, period_extent_first = shape
    ylength = owned_height_lines * row_count
    zlength = owned_depth_slices * col_count
    normal_factor = 1.0 / (period_extent_first * ylength * zlength)
    xpiece = period_extent_first // row_count
    ypiece = ylength // col_count
    zeigen = eigen_row(zlength, 0, zlength)
    yeigen = eigen_row(ypiece, lax.axis_index("col") * ypiece, ylength)
    xeigen = eigen_row(xpiece, lax.axis_index("row") * xpiece, period_extent_first)
    mixed_eigen = (yeigen[:, None] + xeigen[None, :]).reshape(-1)
    return normal_factor / (SMOOTHING * (zeigen[:, None] + mixed_eigen[None, :]) + ANCHOR)


def transform_forward(residual, tables, partial):
    xtable, ytable, ztable = tables
    row_count = lax.axis_size("row")
    components, owned_height_lines, owned_depth_slices, period_extent_first = residual.shape
    ylength = owned_height_lines * row_count
    xpiece = period_extent_first // row_count
    if partial is not None:
        residual = with_pulse(residual, partial, 3)
    spectrum = jnp.einsum("kx,cyzx->cykz", xtable, residual, precision=PRECISE).reshape(
        residual.shape[0], owned_height_lines, period_extent_first * owned_depth_slices
    )
    if partial is None:
        spectrum, _ = exchange(spectrum, None, "row", 2, 1)
        lines = spectrum.reshape(components, ylength, xpiece, owned_depth_slices)
    else:
        spectrum, partial = carried(spectrum, "row", 2, 1)
        lines = with_pulse(
            spectrum.reshape(components, ylength, xpiece, owned_depth_slices), partial, 1
        )
    spectrum = jnp.einsum("ky,cyxz->czkx", ytable, lines, precision=PRECISE).reshape(
        lines.shape[0], owned_depth_slices, ylength * xpiece
    )
    if partial is None:
        spectrum, _ = exchange(spectrum, None, "col", 2, 1)
    else:
        spectrum, partial = carried(spectrum, "col", 2, 1)
    return jnp.einsum("kz,czm->ckm", ztable, spectrum, precision=PRECISE), partial


def transform_inverse(filtered, tables, partial, shape):
    xtable, ytable, ztable = tables
    row_count = lax.axis_size("row")
    col_count = lax.axis_size("col")
    components, owned_height_lines, owned_depth_slices, period_extent_first = shape
    ylength = owned_height_lines * row_count
    xpiece = period_extent_first // row_count
    zwide = widened(ztable, col_count)
    ywide = widened(ytable, row_count)
    spectrum = jnp.einsum(
        "kz,czm->ckm", zwide, with_pulse(filtered, partial, 1), precision=PRECISE
    )
    spectrum, partial = carried(spectrum, "col", 1, 2)
    lines = with_pulse(
        spectrum.reshape(components, owned_depth_slices + 2, ylength, xpiece), partial, 2
    )
    spectrum = jnp.einsum("ky,czyx->ckxz", ywide, lines, precision=PRECISE).reshape(
        components + 1, row_count * (owned_height_lines + 2), xpiece * (owned_depth_slices + 2)
    )
    spectrum, partial = carried(spectrum, "row", 1, 2)
    return jnp.einsum(
        "kx,cyxz->cyzk",
        xtable,
        spectrum.reshape(
            components, owned_height_lines + 2, period_extent_first, owned_depth_slices + 2
        ),
        precision=PRECISE,
    ), partial


def forward(extended, direction):
    owned_height_lines = extended.shape[-3] - 2
    owned_depth_slices = extended.shape[-2] - 2
    root = extended[..., : owned_height_lines + 1, : owned_depth_slices + 1, :]
    if direction == 0:
        return jnp.roll(root, -1, -1) - root
    if direction == 1:
        return extended[..., 1 : owned_height_lines + 2, : owned_depth_slices + 1, :] - root
    return extended[..., : owned_height_lines + 1, 1 : owned_depth_slices + 2, :] - root


def backward(region, direction):
    center = region[..., 1:, 1:, :]
    if direction == 0:
        return center - jnp.roll(center, 1, -1)
    if direction == 1:
        return center - region[..., :-1, 1:, :]
    return center - region[..., 1:, :-1, :]


def extend(field):
    return padded(field, (("row", 1), ("col", 2)), 1)


def lower_region(pressure):
    below_y = from_behind(pressure[-1:], "row", 1)
    below_z = from_behind(pressure[:, -1:], "col", 1)
    corner = jnp.zeros((1, 1, pressure.shape[2]), jnp.float32)
    upper_band = jnp.concatenate([corner, below_y], 1)
    main_band = jnp.concatenate([below_z, pressure], 1)
    return jnp.concatenate([upper_band, main_band], 0)


def operate(extended, shear_resistance_map):
    owned_height_lines = extended.shape[1] - 2
    owned_depth_slices = extended.shape[2] - 2
    gradients = [[forward(extended[target], source) for source in range(3)] for target in range(3)]
    spread = gradients[0][0] + gradients[1][1] + gradients[2][2]
    result = []
    for target in range(3):
        summed = (
            ANCHOR * extended[target, 1 : owned_height_lines + 1, 1 : owned_depth_slices + 1, :]
        )
        for source in range(3):
            fluxes = shear_resistance_map * (gradients[target][source] + gradients[source][target])
            if target == source:
                fluxes = fluxes + AUGMENT * spread
            summed = summed - backward(fluxes, source)
        result.append(summed)
    return jnp.stack(result)


def pressure_gradient(region):
    return jnp.stack([-backward(region, target) for target in range(3)])


def divergence_region(extended):
    return forward(extended[0], 0) + forward(extended[1], 1) + forward(extended[2], 2)


def per_device(prior_window_motion, prior_window_stress, heat_scalar):
    owned_height_lines, owned_depth_slices, period_extent_first = heat_scalar.shape
    tables = (
        cas_matrix(period_extent_first),
        cas_matrix(owned_height_lines * lax.axis_size("row")),
        cas_matrix(owned_depth_slices * lax.axis_size("col")),
    )
    stacked_fields = jnp.concatenate(
        [prior_window_motion, prior_window_stress[None], heat_scalar[None]], 0
    )
    extended = padded(stacked_fields, (("row", 1), ("col", 2)), 1)
    shear_resistance_map = jnp.exp(
        ENABLE_SWITCH
        * (
            1.0
            / (extended[4, : owned_height_lines + 1, : owned_depth_slices + 1, :] + OFFSET_COUNT)
            - 1.0 / (0.5 + OFFSET_COUNT)
        )
    )
    thermal_lift = RAYLEIGH_NUMBER * (heat_scalar - 0.5)
    zeroes = jnp.zeros_like(thermal_lift)
    forcing = jnp.stack([zeroes, zeroes, thermal_lift])
    velocity_ext = extended[0:3]
    pressure_low = extended[3, : owned_height_lines + 1, : owned_depth_slices + 1, :]
    symbol = spectral_symbol(prior_window_motion.shape)
    inner_cells = (slice(None), slice(1, owned_height_lines + 1), slice(1, owned_depth_slices + 1))
    for outer_step in range(OUTER):
        pushing = pressure_gradient(pressure_low)
        residual = forcing - pushing - operate(velocity_ext, shear_resistance_map)
        spectrum, _ = transform_forward(residual, tables, None)
        direction_ext = None
        energy_now = jnp.float32(1.0)
        for inner_step in range(INNER):
            if inner_step > 0:
                image_spectrum, curvature = transform_forward(image, tables, curvature_part)
                step_size = energy_now / curvature
                velocity_ext = velocity_ext + step_size * direction_ext
                spectrum = spectrum - step_size * image_spectrum
            filtered = spectrum * symbol[None]
            precond_ext, energy_next = transform_inverse(
                filtered, tables, jnp.sum(spectrum * filtered), prior_window_motion.shape
            )
            if inner_step == 0:
                direction_ext = precond_ext
            else:
                direction_ext = precond_ext + energy_next / energy_now * direction_ext
            energy_now = energy_next
            image = operate(direction_ext, shear_resistance_map)
            curvature_part = jnp.sum(direction_ext[inner_cells] * image)
        step_size = energy_now / global_sum(curvature_part)
        velocity_ext = velocity_ext + step_size * direction_ext
        spread_now = divergence_region(velocity_ext)
        pressure_low = pressure_low + AUGMENT * spread_now
    velocity = velocity_ext[:, 1 : owned_height_lines + 1, 1 : owned_depth_slices + 1, :]
    pressure = pressure_low[1:, 1:, :]
    return (velocity, pressure)


def solution(mesh):
    placed = (P(None, "row", "col", None), P("row", "col", None), P("row", "col", None))
    return jax.shard_map(
        per_device,
        mesh=mesh,
        in_specs=placed,
        out_specs=(P(None, "row", "col", None), P("row", "col", None)),
        check_vma=False,
    )
```
